128 devices in a mesh: row: 16 (over x, y_hi, core), col: 8 (over z, y_lo).
Axes of the slice: x: 4, y: 4 (y_hi: 2, y_lo: 2; y = y_hi * 2 + y_lo), z: 4, core: 2. Of those that a mesh axis runs over, the one named last changes fastest.
Arguments:
- band_cells: float32 [3, 1024, 2], P(None, ('row', 'col')), may hold values from 0 to 1
- cell_counts: int32 [1024], P(('row', 'col')), may hold values from 1 to 2, as said below
- cell_assign: int32 [1024], P(('row', 'col')), may hold values from 0 to 1023, as said below
- wake_pos: float32 [3, 1048576], P(None, ('row', 'col')), may hold values from 0 to 1
- wake_strength: float32 [3, 1048576], P(None, ('row', 'col')), may hold values from -0.005859375 to 0.005859375
- wake_core: float32 [1, 1048576], P(None, ('row', 'col')), may hold values from 0.05 to 0.15
Outputs:
- velocity: float32 [3, 1024, 2], P(None, ('row', 'col'))
- gradient: float32 [9, 1024, 2], P(None, ('row', 'col'))
The draws below stay inside these ranges and needn't reach their ends.
Inputs may be any that keep to these rules, and one draw needn't show every extreme that they name: `cell_counts`: each band cell holds its live particles in its first slots; some cell is full in every draw. `cell_assign`: A permutation of the cells. The cells of the device with index d along row+col go to positions q with q // 64 == d // 8; at most 1 of them land in the positions of any one device (q // 8); where 8 is a multiple of 8, exactly 1 land in the positions of each device of the group, else some pair of devices reaches 1.
All inputs are finite; a program needn't handle non-finite values.
Results may differ from the reference program's by a relative error of at most 0.0003.
Values sent between devices are 32-bit elements; how exact they have to be, the bound alone decides.
No kernel may reach another device: no remote copies, remote signals or barrier semaphores. Data moves between devices by JAX's collectives and lax.ppermute only.
A program may use at most 64 MiB of HBM per device.

```python
import math
import jax
import jax.numpy as jnp
from jax import lax

CAP = 2
TILE_DEV = 8
GROUP_DEVS = 8
ROW_DEVS = 16
CELLS = 1024
SOURCES = 1048576


def draw_cell_counts(key, part):
    values_drawn = jax.random.randint(key, (CELLS,), 1, CAP + 1)
    full_index = jax.random.randint(jax.random.fold_in(key, 1), (), 0, CELLS)
    return values_drawn.at[full_index].set(CAP).astype(jnp.int32)


def draw_cell_assign(key, part):
    cell_ids = jnp.arange(CELLS, dtype=jnp.int32)
    device_ids = cell_ids // TILE_DEV
    within = cell_ids % TILE_DEV
    group_ids = device_ids // GROUP_DEVS
    col_ids = device_ids % GROUP_DEVS
    offsets = jax.random.permutation(jax.random.fold_in(key, 11), GROUP_DEVS).astype(jnp.int32)
    relabel_in = jax.vmap(lambda sub: jax.random.permutation(sub, GROUP_DEVS))(jax.random.split(jax.random.fold_in(key, 12), ROW_DEVS)).astype(jnp.int32)
    relabel_out = jax.vmap(lambda sub: jax.random.permutation(sub, GROUP_DEVS))(jax.random.split(jax.random.fold_in(key, 13), ROW_DEVS)).astype(jnp.int32)
    slot_order = jax.vmap(lambda sub: jax.random.permutation(sub, TILE_DEV))(jax.random.split(jax.random.fold_in(key, 14), ROW_DEVS)).astype(jnp.int32)
    shifted = (relabel_in[group_ids, col_ids] + offsets[within % GROUP_DEVS]) % GROUP_DEVS
    target_dev = relabel_out[group_ids, shifted]
    return ((group_ids * GROUP_DEVS + target_dev) * TILE_DEV + slot_order[group_ids, within]).astype(jnp.int32)


def block_scale(key, extent, cuts, least, high):
    gain = 1.0
    for dim, parts in cuts:
        heights = jax.random.uniform(jax.random.fold_in(jax.random.fold_in(key, 6), dim), (parts,), jnp.float32, least / len(cuts), high / len(cuts))
        gain = gain * jnp.repeat(jnp.exp(heights), extent[dim] // parts).reshape((-1,) + (1,) * (len(extent) - 1 - dim))
    return gain


def gaussian(stream_key, dims, width, limit, shards=(), held_as=jnp.bfloat16):
    drawn = jax.random.normal(stream_key, dims, jnp.float32) * width
    if len(shards) > 0:
        drawn = block_scale(stream_key, dims, shards, -0.22, 0.18) * drawn
    return jnp.clip(drawn, min=-limit, max=limit).astype(held_as)


def setup_inputs(seed: int = 0) -> dict:
    streams_of = jax.random.split(jax.random.key(seed), 7)
    band_cells = jnp.clip(1.0 * jax.random.uniform(streams_of[0], (3, CELLS, CAP), jnp.float32) ** block_scale(streams_of[0], (3, CELLS, CAP), ((1, 128),), -0.2, 0.2), 0.0, 1.0)
    cell_counts = draw_cell_counts(jax.random.fold_in(streams_of[6], 71), 0)
    cell_assign = draw_cell_assign(jax.random.fold_in(streams_of[6], 71), 0)
    wake_pos = jnp.clip(1.0 * jax.random.uniform(streams_of[3], (3, SOURCES), jnp.float32) ** block_scale(streams_of[3], (3, SOURCES), ((1, 128),), -0.2, 0.2), 0.0, 1.0)
    wake_strength = gaussian(streams_of[4], (3, SOURCES), SOURCES ** -0.5, 0.005859375, ((1, 128),), jnp.float32)
    wake_core = jnp.clip(jnp.exp(math.log(0.15) - 1.0986123 * jax.random.uniform(streams_of[5], (1, SOURCES), jnp.float32) ** block_scale(streams_of[5], (1, SOURCES), ((1, 128),), -0.2, 0.2)), 0.05, 0.15)
    return dict(band_cells=band_cells, cell_counts=cell_counts, cell_assign=cell_assign, wake_pos=wake_pos, wake_strength=wake_strength, wake_core=wake_core)


def block_sums(target_pos, source_pos, source_str, source_core):
    delta_x = target_pos[0][:, None] - source_pos[0][None, :]
    delta_y = target_pos[1][:, None] - source_pos[1][None, :]
    delta_z = target_pos[2][:, None] - source_pos[2][None, :]
    radius_sq = delta_x * delta_x + delta_y * delta_y + delta_z * delta_z + source_core[0][None, :] * source_core[0][None, :]
    inverse = lax.rsqrt(radius_sq)
    kernel_three = inverse * inverse * inverse
    kernel_five = kernel_three * inverse * inverse
    alpha_x = source_str[0][None, :]
    alpha_y = source_str[1][None, :]
    alpha_z = source_str[2][None, :]
    cross_x = delta_y * alpha_z - delta_z * alpha_y
    cross_y = delta_z * alpha_x - delta_x * alpha_z
    cross_z = delta_x * alpha_y - delta_y * alpha_x
    terms_list = [kernel_three * cross_x, kernel_three * cross_y, kernel_three * cross_z, kernel_three * alpha_x, kernel_three * alpha_y, kernel_three * alpha_z]
    for along in (delta_x, delta_y, delta_z):
        for cross in (cross_x, cross_y, cross_z):
            terms_list.append(kernel_five * along * cross)
    return jnp.stack([lax.optimization_barrier(jnp.sum(term, axis=1)) for term in terms_list])

def pair_sums(target_pos, source_pos, source_str, source_core, block_width):
    block_steps = source_pos.shape[1] // block_width

    def one_block(running, block_index):
        offset = block_index * block_width
        part_pos = lax.dynamic_slice_in_dim(source_pos, offset, block_width, 1)
        part_str = lax.dynamic_slice_in_dim(source_str, offset, block_width, 1)
        part_core = lax.dynamic_slice_in_dim(source_core, offset, block_width, 1)
        return (running + block_sums(target_pos, part_pos, part_str, part_core), None)
    start_sums = jnp.zeros((15, target_pos.shape[1]), jnp.float32)
    running, unused = lax.scan(one_block, start_sums, jnp.arange(block_steps, dtype=jnp.int32))
    return running

def finish(kernel_sums, slot_counts, slot_cap):
    biot_scale = -1.0 / (4.0 * math.pi)
    swirl_x, swirl_y, swirl_z = (kernel_sums[3], kernel_sums[4], kernel_sums[5])
    zero_row = jnp.zeros_like(swirl_x)
    levi_terms = [[zero_row, swirl_z, -swirl_y], [-swirl_z, zero_row, swirl_x], [swirl_y, -swirl_x, zero_row]]
    grad_rows = []
    for comp_m in range(3):
        for comp_n in range(3):
            grad_rows.append(biot_scale * (levi_terms[comp_m][comp_n] - 3.0 * kernel_sums[6 + comp_n * 3 + comp_m]))
    slot_ids = jnp.arange(slot_cap).astype(slot_counts.dtype)
    alive_mask = (slot_ids[None, :] < slot_counts[:, None]).astype(jnp.float32).reshape(-1)
    velocity = biot_scale * kernel_sums[0:3] * alive_mask[None, :]
    gradient = jnp.stack(grad_rows) * alive_mask[None, :]
    cell_total = slot_counts.shape[0]
    return (velocity.reshape(3, cell_total, slot_cap), gradient.reshape(9, cell_total, slot_cap))

def reference(band_cells, cell_counts, cell_assign, wake_pos, wake_strength, wake_core):
    relaid_cells = jnp.zeros_like(band_cells).at[:, cell_assign, :].set(band_cells)
    relaid_counts = jnp.zeros_like(cell_counts).at[cell_assign].set(cell_counts)
    target_pos = relaid_cells.reshape(3, -1)
    block_width = math.gcd(wake_pos.shape[1], 4096)
    kernel_sums = pair_sums(target_pos, wake_pos, wake_strength, wake_core, block_width)
    return finish(kernel_sums, relaid_counts, band_cells.shape[2])
```

```python
import math

import jax
import jax.numpy as jnp
from jax import lax
from jax.sharding import PartitionSpec as P

HIGHEST = lax.Precision.HIGHEST


def block_sums(target_pos, source_pos, source_str, source_core):
    delta_x = target_pos[0][:, None] - source_pos[0][None, :]
    delta_y = target_pos[1][:, None] - source_pos[1][None, :]
    delta_z = target_pos[2][:, None] - source_pos[2][None, :]
    radius_sq = (
        delta_x * delta_x
        + delta_y * delta_y
        + delta_z * delta_z
        + source_core[0][None, :] * source_core[0][None, :]
    )
    inverse = lax.rsqrt(radius_sq)
    kernel_three = inverse * inverse * inverse
    kernel_five = kernel_three * inverse * inverse
    alpha_x = source_str[0][None, :]
    alpha_y = source_str[1][None, :]
    alpha_z = source_str[2][None, :]
    cross_x = delta_y * alpha_z - delta_z * alpha_y
    cross_y = delta_z * alpha_x - delta_x * alpha_z
    cross_z = delta_x * alpha_y - delta_y * alpha_x
    terms_list = [
        kernel_three * cross_x,
        kernel_three * cross_y,
        kernel_three * cross_z,
        kernel_three * alpha_x,
        kernel_three * alpha_y,
        kernel_three * alpha_z,
    ]
    for along in (delta_x, delta_y, delta_z):
        for cross in (cross_x, cross_y, cross_z):
            terms_list.append(kernel_five * along * cross)
    return jnp.stack([jnp.sum(term, axis=1) for term in terms_list])


def pair_sums(target_pos, source_pos, source_str, source_core):
    source_total = source_pos.shape[1]
    block_width = math.gcd(source_total, max(512, 1048576 // target_pos.shape[1]))
    block_steps = source_total // block_width

    def one_block(running, block_index):
        offset = block_index * block_width
        part_pos = lax.dynamic_slice_in_dim(source_pos, offset, block_width, 1)
        part_str = lax.dynamic_slice_in_dim(source_str, offset, block_width, 1)
        part_core = lax.dynamic_slice_in_dim(source_core, offset, block_width, 1)
        return (running + block_sums(target_pos, part_pos, part_str, part_core), None)

    start_sums = jnp.zeros((15, target_pos.shape[1]), jnp.float32)
    running, unused = lax.scan(one_block, start_sums, jnp.arange(block_steps, dtype=jnp.int32))
    return running


def combine_rows(kernel_sums):
    biot_scale = -1.0 / (4.0 * math.pi)
    swirl_x, swirl_y, swirl_z = (kernel_sums[3], kernel_sums[4], kernel_sums[5])
    zero_row = jnp.zeros_like(swirl_x)
    levi_terms = [
        [zero_row, swirl_z, -swirl_y],
        [-swirl_z, zero_row, swirl_x],
        [swirl_y, -swirl_x, zero_row],
    ]
    out_rows = [
        biot_scale * kernel_sums[0],
        biot_scale * kernel_sums[1],
        biot_scale * kernel_sums[2],
    ]
    for comp_m in range(3):
        for comp_n in range(3):
            out_rows.append(
                biot_scale
                * (levi_terms[comp_m][comp_n] - 3.0 * kernel_sums[6 + comp_n * 3 + comp_m])
            )
    return jnp.stack(out_rows)


def apply_mask(finished_rows, slot_counts, slot_cap):
    slot_ids = jnp.arange(slot_cap).astype(slot_counts.dtype)
    alive_mask = (slot_ids[None, :] < slot_counts[:, None]).astype(jnp.float32).reshape(-1)
    masked = finished_rows * alive_mask[None, :]
    cell_total = slot_counts.shape[0]
    return (
        masked[0:3].reshape(3, cell_total, slot_cap),
        masked[3:12].reshape(9, cell_total, slot_cap),
    )


def per_device(band_cells, cell_counts, cell_assign, wake_pos, wake_strength, wake_core):
    axes = ("row", "col")
    col_devs = lax.axis_size("col")
    cell_total = band_cells.shape[1]
    slot_cap = band_cells.shape[2]
    group_cells = cell_total * col_devs
    packed = jnp.concatenate(
        [
            band_cells.transpose(1, 0, 2).reshape(cell_total, 3 * slot_cap),
            cell_counts.astype(jnp.float32)[:, None],
            cell_assign.astype(jnp.float32)[:, None],
        ],
        axis=1,
    )
    every_cell = lax.all_gather(packed, axes, axis=0, tiled=True)
    all_cells = every_cell.shape[0]
    groups = all_cells // group_cells
    grouped = every_cell.reshape(groups, group_cells, 3 * slot_cap + 2)
    within = grouped[:, :, -1].astype(jnp.int32) % group_cells
    position = jnp.arange(group_cells, dtype=jnp.int32)
    chosen = within[:, None, :] == position[None, :, None]
    relaid = jnp.sum(
        jnp.where(chosen[:, :, :, None], grouped[:, None, :, : 3 * slot_cap + 1], 0.0), axis=2
    ).reshape(all_cells, 3 * slot_cap + 1)
    target_pos = relaid[:, : 3 * slot_cap].reshape(all_cells, 3, slot_cap)
    target_pos = target_pos.transpose(1, 0, 2).reshape(3, all_cells * slot_cap)
    device = lax.axis_index("row") * col_devs + lax.axis_index("col")
    own_counts = lax.dynamic_slice_in_dim(relaid[:, 3 * slot_cap], device * cell_total, cell_total)
    local_sums = pair_sums(target_pos, wake_pos, wake_strength, wake_core)
    own_rows = lax.psum_scatter(local_sums, axes, scatter_dimension=1, tiled=True)
    finished_rows = combine_rows(own_rows)
    return apply_mask(finished_rows, own_counts, slot_cap)


def solution(mesh):
    placed = (
        P(None, ("row", "col"), None),
        P(("row", "col")),
        P(("row", "col")),
        P(None, ("row", "col")),
        P(None, ("row", "col")),
        P(None, ("row", "col")),
    )
    return jax.shard_map(
        per_device,
        mesh=mesh,
        in_specs=placed,
        out_specs=(P(None, ("row", "col"), None), P(None, ("row", "col"), None)),
        check_vma=False,
    )
```

```python
import math

import jax
import jax.numpy as jnp
from jax import lax
from jax.sharding import PartitionSpec as P

HIGHEST = lax.Precision.HIGHEST


def block_sums(target_pos, source_pos, source_str, source_core):
    delta_x = target_pos[0][:, None] - source_pos[0][None, :]
    delta_y = target_pos[1][:, None] - source_pos[1][None, :]
    delta_z = target_pos[2][:, None] - source_pos[2][None, :]
    radius_sq = (
        delta_x * delta_x
        + delta_y * delta_y
        + delta_z * delta_z
        + source_core[0][None, :] * source_core[0][None, :]
    )
    inverse = lax.rsqrt(radius_sq)
    kernel_three = inverse * inverse * inverse
    kernel_five = kernel_three * inverse * inverse
    alpha_x = source_str[0][None, :]
    alpha_y = source_str[1][None, :]
    alpha_z = source_str[2][None, :]
    cross_x = delta_y * alpha_z - delta_z * alpha_y
    cross_y = delta_z * alpha_x - delta_x * alpha_z
    cross_z = delta_x * alpha_y - delta_y * alpha_x
    terms_list = [
        kernel_three * cross_x,
        kernel_three * cross_y,
        kernel_three * cross_z,
        kernel_three * alpha_x,
        kernel_three * alpha_y,
        kernel_three * alpha_z,
    ]
    for along in (delta_x, delta_y, delta_z):
        for cross in (cross_x, cross_y, cross_z):
            terms_list.append(kernel_five * along * cross)
    return jnp.stack([jnp.sum(term, axis=1) for term in terms_list])


def pair_sums(target_pos, source_pos, source_str, source_core):
    source_total = source_pos.shape[1]
    block_width = math.gcd(source_total, max(512, 1048576 // target_pos.shape[1]))
    block_steps = source_total // block_width

    def one_block(running, block_index):
        offset = block_index * block_width
        part_pos = lax.dynamic_slice_in_dim(source_pos, offset, block_width, 1)
        part_str = lax.dynamic_slice_in_dim(source_str, offset, block_width, 1)
        part_core = lax.dynamic_slice_in_dim(source_core, offset, block_width, 1)
        return (running + block_sums(target_pos, part_pos, part_str, part_core), None)

    start_sums = jnp.zeros((15, target_pos.shape[1]), jnp.float32)
    running, unused = lax.scan(one_block, start_sums, jnp.arange(block_steps, dtype=jnp.int32))
    return running


def combine_rows(kernel_sums):
    biot_scale = -1.0 / (4.0 * math.pi)
    swirl_x, swirl_y, swirl_z = (kernel_sums[3], kernel_sums[4], kernel_sums[5])
    zero_row = jnp.zeros_like(swirl_x)
    levi_terms = [
        [zero_row, swirl_z, -swirl_y],
        [-swirl_z, zero_row, swirl_x],
        [swirl_y, -swirl_x, zero_row],
    ]
    out_rows = [
        biot_scale * kernel_sums[0],
        biot_scale * kernel_sums[1],
        biot_scale * kernel_sums[2],
    ]
    for comp_m in range(3):
        for comp_n in range(3):
            out_rows.append(
                biot_scale
                * (levi_terms[comp_m][comp_n] - 3.0 * kernel_sums[6 + comp_n * 3 + comp_m])
            )
    return jnp.stack(out_rows)


def apply_mask(finished_rows, slot_counts, slot_cap):
    slot_ids = jnp.arange(slot_cap).astype(slot_counts.dtype)
    alive_mask = (slot_ids[None, :] < slot_counts[:, None]).astype(jnp.float32).reshape(-1)
    masked = finished_rows * alive_mask[None, :]
    cell_total = slot_counts.shape[0]
    return (
        masked[0:3].reshape(3, cell_total, slot_cap),
        masked[3:12].reshape(9, cell_total, slot_cap),
    )


def per_device(band_cells, cell_counts, cell_assign, wake_pos, wake_strength, wake_core):
    axes = ("row", "col")
    col_devs = lax.axis_size("col")
    cell_total = band_cells.shape[1]
    slot_cap = band_cells.shape[2]
    group_cells = cell_total * col_devs
    packed = jnp.concatenate(
        [
            band_cells.transpose(1, 0, 2).reshape(cell_total, 3 * slot_cap),
            cell_counts.astype(jnp.float32)[:, None],
            cell_assign.astype(jnp.float32)[:, None],
        ],
        axis=1,
    )
    devices = lax.axis_size("row") * col_devs
    copies = jnp.broadcast_to(packed[None], (devices,) + packed.shape)
    every_cell = lax.all_to_all(copies, axes, 0, 0, tiled=True)
    all_cells = devices * cell_total
    every_cell = every_cell.reshape(all_cells, packed.shape[1])
    groups = all_cells // group_cells
    grouped = every_cell.reshape(groups, group_cells, 3 * slot_cap + 2)
    within = grouped[:, :, -1].astype(jnp.int32) % group_cells
    position = jnp.arange(group_cells, dtype=jnp.int32)
    chosen = within[:, None, :] == position[None, :, None]
    relaid = jnp.sum(
        jnp.where(chosen[:, :, :, None], grouped[:, None, :, : 3 * slot_cap + 1], 0.0), axis=2
    ).reshape(all_cells, 3 * slot_cap + 1)
    target_pos = relaid[:, : 3 * slot_cap].reshape(all_cells, 3, slot_cap)
    target_pos = target_pos.transpose(1, 0, 2).reshape(3, all_cells * slot_cap)
    device = lax.axis_index("row") * col_devs + lax.axis_index("col")
    own_counts = lax.dynamic_slice_in_dim(relaid[:, 3 * slot_cap], device * cell_total, cell_total)
    local_sums = pair_sums(target_pos, wake_pos, wake_strength, wake_core)
    rows = local_sums.shape[0]
    by_device = local_sums.reshape(rows, devices, cell_total * slot_cap).transpose(1, 0, 2)
    own_rows = jnp.sum(lax.all_to_all(by_device, axes, 0, 0, tiled=True), axis=0)
    finished_rows = combine_rows(own_rows)
    return apply_mask(finished_rows, own_counts, slot_cap)


def solution(mesh):
    placed = (
        P(None, ("row", "col"), None),
        P(("row", "col")),
        P(("row", "col")),
        P(None, ("row", "col")),
        P(None, ("row", "col")),
        P(None, ("row", "col")),
    )
    return jax.shard_map(
        per_device,
        mesh=mesh,
        in_specs=placed,
        out_specs=(P(None, ("row", "col"), None), P(None, ("row", "col"), None)),
        check_vma=False,
    )
```

```python
import math

import jax
import jax.numpy as jnp
from jax import lax
from jax.experimental import pallas as pl
from jax.experimental.pallas import tpu as pltpu
from jax.sharding import PartitionSpec as P

HIGHEST = lax.Precision.HIGHEST


def block_sums(target_pos, source_pos, source_str, source_core):
    delta_x = target_pos[0][:, None] - source_pos[0][None, :]
    delta_y = target_pos[1][:, None] - source_pos[1][None, :]
    delta_z = target_pos[2][:, None] - source_pos[2][None, :]
    radius_sq = (
        delta_x * delta_x
        + delta_y * delta_y
        + delta_z * delta_z
        + source_core[0][None, :] * source_core[0][None, :]
    )
    inverse = lax.rsqrt(radius_sq)
    kernel_three = inverse * inverse * inverse
    kernel_five = kernel_three * inverse * inverse
    alpha_x = source_str[0][None, :]
    alpha_y = source_str[1][None, :]
    alpha_z = source_str[2][None, :]
    cross_x = delta_y * alpha_z - delta_z * alpha_y
    cross_y = delta_z * alpha_x - delta_x * alpha_z
    cross_z = delta_x * alpha_y - delta_y * alpha_x
    terms_list = [
        kernel_three * cross_x,
        kernel_three * cross_y,
        kernel_three * cross_z,
        kernel_three * alpha_x,
        kernel_three * alpha_y,
        kernel_three * alpha_z,
    ]
    for along in (delta_x, delta_y, delta_z):
        for cross in (cross_x, cross_y, cross_z):
            terms_list.append(kernel_five * along * cross)
    return jnp.stack([jnp.sum(term, axis=1) for term in terms_list])


def pair_kernel(source_ref, target_ref, out_ref):
    source_total = source_ref.shape[1]
    target_x = target_ref[0]
    target_y = target_ref[1]
    target_z = target_ref[2]

    def one_source(index, running):
        delta_x = target_x - source_ref[0, index]
        delta_y = target_y - source_ref[1, index]
        delta_z = target_z - source_ref[2, index]
        alpha_x = source_ref[3, index]
        alpha_y = source_ref[4, index]
        alpha_z = source_ref[5, index]
        radius_sq = delta_x * delta_x + delta_y * delta_y + delta_z * delta_z + source_ref[6, index]
        inverse = lax.rsqrt(radius_sq)
        inverse_sq = inverse * inverse
        kernel_three = inverse_sq * inverse
        kernel_five = kernel_three * inverse_sq
        cross_x = delta_y * alpha_z - delta_z * alpha_y
        cross_y = delta_z * alpha_x - delta_x * alpha_z
        cross_z = delta_x * alpha_y - delta_y * alpha_x
        five_x = kernel_five * cross_x
        five_y = kernel_five * cross_y
        five_z = kernel_five * cross_z
        terms = [
            kernel_three * cross_x,
            kernel_three * cross_y,
            kernel_three * cross_z,
            kernel_three * alpha_x,
            kernel_three * alpha_y,
            kernel_three * alpha_z,
        ]
        for along in (delta_x, delta_y, delta_z):
            terms.extend([along * five_x, along * five_y, along * five_z])
        return tuple(total + term for total, term in zip(running, terms))

    start = tuple(jnp.zeros_like(target_x) for _ in range(15))
    running = lax.fori_loop(0, source_total, one_source, start, unroll=4)
    for row in range(15):
        out_ref[row] = running[row]


def pair_sums(target_pos, source_pos, source_str, source_core):
    target_total = target_pos.shape[1]
    sublanes = target_total // 128
    tile = 8 if sublanes % 8 == 0 else sublanes
    sources = jnp.concatenate(
        [source_pos, source_str, source_core * source_core, jnp.zeros_like(source_core)], axis=0
    )
    targets = target_pos.reshape(3, sublanes, 128)
    sums = pl.pallas_call(
        pair_kernel,
        grid=(sublanes // tile,),
        in_specs=[
            pl.BlockSpec(memory_space=pltpu.SMEM),
            pl.BlockSpec((3, tile, 128), lambda step: (0, step, 0)),
        ],
        out_specs=pl.BlockSpec((15, tile, 128), lambda step: (0, step, 0)),
        out_shape=jax.ShapeDtypeStruct((15, sublanes, 128), jnp.float32),
    )(sources, targets)
    return sums.reshape(15, target_total)


def combine_rows(kernel_sums):
    biot_scale = -1.0 / (4.0 * math.pi)
    swirl_x, swirl_y, swirl_z = (kernel_sums[3], kernel_sums[4], kernel_sums[5])
    zero_row = jnp.zeros_like(swirl_x)
    levi_terms = [
        [zero_row, swirl_z, -swirl_y],
        [-swirl_z, zero_row, swirl_x],
        [swirl_y, -swirl_x, zero_row],
    ]
    out_rows = [
        biot_scale * kernel_sums[0],
        biot_scale * kernel_sums[1],
        biot_scale * kernel_sums[2],
    ]
    for comp_m in range(3):
        for comp_n in range(3):
            out_rows.append(
                biot_scale
                * (levi_terms[comp_m][comp_n] - 3.0 * kernel_sums[6 + comp_n * 3 + comp_m])
            )
    return jnp.stack(out_rows)


def apply_mask(finished_rows, slot_counts, slot_cap):
    slot_ids = jnp.arange(slot_cap).astype(slot_counts.dtype)
    alive_mask = (slot_ids[None, :] < slot_counts[:, None]).astype(jnp.float32).reshape(-1)
    masked = finished_rows * alive_mask[None, :]
    cell_total = slot_counts.shape[0]
    return (
        masked[0:3].reshape(3, cell_total, slot_cap),
        masked[3:12].reshape(9, cell_total, slot_cap),
    )


def per_device(band_cells, cell_counts, cell_assign, wake_pos, wake_strength, wake_core):
    axes = ("row", "col")
    col_devs = lax.axis_size("col")
    cell_total = band_cells.shape[1]
    slot_cap = band_cells.shape[2]
    group_cells = cell_total * col_devs
    packed = jnp.concatenate(
        [
            band_cells.transpose(1, 0, 2).reshape(cell_total, 3 * slot_cap),
            cell_counts.astype(jnp.float32)[:, None],
            cell_assign.astype(jnp.float32)[:, None],
        ],
        axis=1,
    )
    devices = lax.axis_size("row") * col_devs
    copies = jnp.broadcast_to(packed[None], (devices,) + packed.shape)
    every_cell = lax.all_to_all(copies, axes, 0, 0, tiled=True)
    all_cells = devices * cell_total
    every_cell = every_cell.reshape(all_cells, packed.shape[1])
    groups = all_cells // group_cells
    grouped = every_cell.reshape(groups, group_cells, 3 * slot_cap + 2)
    within = grouped[:, :, -1].astype(jnp.int32) % group_cells
    position = jnp.arange(group_cells, dtype=jnp.int32)
    chosen = within[:, None, :] == position[None, :, None]
    relaid = jnp.sum(
        jnp.where(chosen[:, :, :, None], grouped[:, None, :, : 3 * slot_cap + 1], 0.0), axis=2
    ).reshape(all_cells, 3 * slot_cap + 1)
    target_pos = relaid[:, : 3 * slot_cap].reshape(all_cells, 3, slot_cap)
    target_pos = target_pos.transpose(1, 0, 2).reshape(3, all_cells * slot_cap)
    device = lax.axis_index("row") * col_devs + lax.axis_index("col")
    own_counts = lax.dynamic_slice_in_dim(relaid[:, 3 * slot_cap], device * cell_total, cell_total)
    local_sums = pair_sums(target_pos, wake_pos, wake_strength, wake_core)
    rows = local_sums.shape[0]
    by_device = local_sums.reshape(rows, devices, cell_total * slot_cap).transpose(1, 0, 2)
    own_rows = jnp.sum(lax.all_to_all(by_device, axes, 0, 0, tiled=True), axis=0)
    finished_rows = combine_rows(own_rows)
    return apply_mask(finished_rows, own_counts, slot_cap)


def solution(mesh):
    placed = (
        P(None, ("row", "col"), None),
        P(("row", "col")),
        P(("row", "col")),
        P(None, ("row", "col")),
        P(None, ("row", "col")),
        P(None, ("row", "col")),
    )
    return jax.shard_map(
        per_device,
        mesh=mesh,
        in_specs=placed,
        out_specs=(P(None, ("row", "col"), None), P(None, ("row", "col"), None)),
        check_vma=False,
    )
```

```python
import math

import jax
import jax.numpy as jnp
from jax import lax
from jax.experimental import pallas as pl
from jax.experimental.pallas import tpu as pltpu
from jax.sharding import PartitionSpec as P

HIGHEST = lax.Precision.HIGHEST


def block_sums(target_pos, source_pos, source_str, source_core):
    delta_x = target_pos[0][:, None] - source_pos[0][None, :]
    delta_y = target_pos[1][:, None] - source_pos[1][None, :]
    delta_z = target_pos[2][:, None] - source_pos[2][None, :]
    radius_sq = (
        delta_x * delta_x
        + delta_y * delta_y
        + delta_z * delta_z
        + source_core[0][None, :] * source_core[0][None, :]
    )
    inverse = lax.rsqrt(radius_sq)
    kernel_three = inverse * inverse * inverse
    kernel_five = kernel_three * inverse * inverse
    alpha_x = source_str[0][None, :]
    alpha_y = source_str[1][None, :]
    alpha_z = source_str[2][None, :]
    cross_x = delta_y * alpha_z - delta_z * alpha_y
    cross_y = delta_z * alpha_x - delta_x * alpha_z
    cross_z = delta_x * alpha_y - delta_y * alpha_x
    terms_list = [
        kernel_three * cross_x,
        kernel_three * cross_y,
        kernel_three * cross_z,
        kernel_three * alpha_x,
        kernel_three * alpha_y,
        kernel_three * alpha_z,
    ]
    for along in (delta_x, delta_y, delta_z):
        for cross in (cross_x, cross_y, cross_z):
            terms_list.append(kernel_five * along * cross)
    return jnp.stack([jnp.sum(term, axis=1) for term in terms_list])


def pair_kernel(source_ref, target_ref, out_ref):
    source_total = source_ref.shape[1]
    halves = 2 if target_ref.shape[1] % 16 == 0 else 1
    part = target_ref.shape[1] // halves
    target_x = [target_ref[0, k * part : (k + 1) * part] for k in range(halves)]
    target_y = [target_ref[1, k * part : (k + 1) * part] for k in range(halves)]
    target_z = [target_ref[2, k * part : (k + 1) * part] for k in range(halves)]

    def one_source(index, running):
        source_x = source_ref[0, index]
        source_y = source_ref[1, index]
        source_z = source_ref[2, index]
        alpha_x = source_ref[3, index]
        alpha_y = source_ref[4, index]
        alpha_z = source_ref[5, index]
        core_sq = source_ref[6, index]
        updated = []
        for k in range(halves):
            delta_x = target_x[k] - source_x
            delta_y = target_y[k] - source_y
            delta_z = target_z[k] - source_z
            radius_sq = delta_x * delta_x + delta_y * delta_y + delta_z * delta_z + core_sq
            inverse = lax.rsqrt(radius_sq)
            inverse_sq = inverse * inverse
            kernel_three = inverse_sq * inverse
            kernel_five = kernel_three * inverse_sq
            cross_x = delta_y * alpha_z - delta_z * alpha_y
            cross_y = delta_z * alpha_x - delta_x * alpha_z
            cross_z = delta_x * alpha_y - delta_y * alpha_x
            five_x = kernel_five * cross_x
            five_y = kernel_five * cross_y
            five_z = kernel_five * cross_z
            terms = [
                kernel_three * cross_x,
                kernel_three * cross_y,
                kernel_three * cross_z,
                kernel_three * alpha_x,
                kernel_three * alpha_y,
                kernel_three * alpha_z,
            ]
            for along in (delta_x, delta_y, delta_z):
                terms.extend([along * five_x, along * five_y, along * five_z])
            mine = running[15 * k : 15 * k + 15]
            updated.extend(total + term for total, term in zip(mine, terms))
        return tuple(updated)

    start = tuple(jnp.zeros_like(target_x[0]) for _ in range(15 * halves))
    running = lax.fori_loop(0, source_total, one_source, start, unroll=16)
    for k in range(halves):
        for row in range(15):
            out_ref[row, k * part : (k + 1) * part] = running[15 * k + row]


def pair_sums(target_pos, source_pos, source_str, source_core):
    target_total = target_pos.shape[1]
    sublanes = target_total // 128
    tile = 16 if sublanes % 16 == 0 else sublanes
    sources = jnp.concatenate(
        [source_pos, source_str, source_core * source_core, jnp.zeros_like(source_core)], axis=0
    )
    targets = target_pos.reshape(3, sublanes, 128)
    sums = pl.pallas_call(
        pair_kernel,
        grid=(sublanes // tile,),
        in_specs=[
            pl.BlockSpec(memory_space=pltpu.SMEM),
            pl.BlockSpec((3, tile, 128), lambda step: (0, step, 0)),
        ],
        out_specs=pl.BlockSpec((15, tile, 128), lambda step: (0, step, 0)),
        out_shape=jax.ShapeDtypeStruct((15, sublanes, 128), jnp.float32),
    )(sources, targets)
    return sums.reshape(15, target_total)


def combine_rows(kernel_sums):
    biot_scale = -1.0 / (4.0 * math.pi)
    swirl_x, swirl_y, swirl_z = (kernel_sums[3], kernel_sums[4], kernel_sums[5])
    zero_row = jnp.zeros_like(swirl_x)
    levi_terms = [
        [zero_row, swirl_z, -swirl_y],
        [-swirl_z, zero_row, swirl_x],
        [swirl_y, -swirl_x, zero_row],
    ]
    out_rows = [
        biot_scale * kernel_sums[0],
        biot_scale * kernel_sums[1],
        biot_scale * kernel_sums[2],
    ]
    for comp_m in range(3):
        for comp_n in range(3):
            out_rows.append(
                biot_scale
                * (levi_terms[comp_m][comp_n] - 3.0 * kernel_sums[6 + comp_n * 3 + comp_m])
            )
    return jnp.stack(out_rows)


def apply_mask(finished_rows, slot_counts, slot_cap):
    slot_ids = jnp.arange(slot_cap).astype(slot_counts.dtype)
    alive_mask = (slot_ids[None, :] < slot_counts[:, None]).astype(jnp.float32).reshape(-1)
    masked = finished_rows * alive_mask[None, :]
    cell_total = slot_counts.shape[0]
    return (
        masked[0:3].reshape(3, cell_total, slot_cap),
        masked[3:12].reshape(9, cell_total, slot_cap),
    )


def per_device(band_cells, cell_counts, cell_assign, wake_pos, wake_strength, wake_core):
    axes = ("row", "col")
    col_devs = lax.axis_size("col")
    cell_total = band_cells.shape[1]
    slot_cap = band_cells.shape[2]
    group_cells = cell_total * col_devs
    packed = jnp.concatenate(
        [
            band_cells.transpose(1, 0, 2).reshape(cell_total, 3 * slot_cap),
            cell_counts.astype(jnp.float32)[:, None],
            cell_assign.astype(jnp.float32)[:, None],
        ],
        axis=1,
    )
    devices = lax.axis_size("row") * col_devs
    copies = jnp.broadcast_to(packed[None], (devices,) + packed.shape)
    every_cell = lax.all_to_all(copies, axes, 0, 0, tiled=True)
    all_cells = devices * cell_total
    every_cell = every_cell.reshape(all_cells, packed.shape[1])
    groups = all_cells // group_cells
    grouped = every_cell.reshape(groups, group_cells, 3 * slot_cap + 2)
    within = grouped[:, :, -1].astype(jnp.int32) % group_cells
    position = jnp.arange(group_cells, dtype=jnp.int32)
    chosen = within[:, None, :] == position[None, :, None]
    relaid = jnp.sum(
        jnp.where(chosen[:, :, :, None], grouped[:, None, :, : 3 * slot_cap + 1], 0.0), axis=2
    ).reshape(all_cells, 3 * slot_cap + 1)
    target_pos = relaid[:, : 3 * slot_cap].reshape(all_cells, 3, slot_cap)
    target_pos = target_pos.transpose(1, 0, 2).reshape(3, all_cells * slot_cap)
    device = lax.axis_index("row") * col_devs + lax.axis_index("col")
    own_counts = lax.dynamic_slice_in_dim(relaid[:, 3 * slot_cap], device * cell_total, cell_total)
    local_sums = pair_sums(target_pos, wake_pos, wake_strength, wake_core)
    rows = local_sums.shape[0]
    by_device = local_sums.reshape(rows, devices, cell_total * slot_cap).transpose(1, 0, 2)
    own_rows = jnp.sum(lax.all_to_all(by_device, axes, 0, 0, tiled=True), axis=0)
    finished_rows = combine_rows(own_rows)
    return apply_mask(finished_rows, own_counts, slot_cap)


def solution(mesh):
    placed = (
        P(None, ("row", "col"), None),
        P(("row", "col")),
        P(("row", "col")),
        P(None, ("row", "col")),
        P(None, ("row", "col")),
        P(None, ("row", "col")),
    )
    return jax.shard_map(
        per_device,
        mesh=mesh,
        in_specs=placed,
        out_specs=(P(None, ("row", "col"), None), P(None, ("row", "col"), None)),
        check_vma=False,
    )
```

```python
import math

import jax
import jax.numpy as jnp
from jax import lax
from jax.experimental import pallas as pl
from jax.experimental.pallas import tpu as pltpu
from jax.sharding import PartitionSpec as P

HIGHEST = lax.Precision.HIGHEST
ROWS = 14


def block_sums(target_pos, source_pos, source_str, source_core):
    delta_x = target_pos[0][:, None] - source_pos[0][None, :]
    delta_y = target_pos[1][:, None] - source_pos[1][None, :]
    delta_z = target_pos[2][:, None] - source_pos[2][None, :]
    radius_sq = (
        delta_x * delta_x
        + delta_y * delta_y
        + delta_z * delta_z
        + source_core[0][None, :] * source_core[0][None, :]
    )
    inverse = lax.rsqrt(radius_sq)
    kernel_three = inverse * inverse * inverse
    kernel_five = kernel_three * inverse * inverse
    alpha_x = source_str[0][None, :]
    alpha_y = source_str[1][None, :]
    alpha_z = source_str[2][None, :]
    cross_x = delta_y * alpha_z - delta_z * alpha_y
    cross_y = delta_z * alpha_x - delta_x * alpha_z
    cross_z = delta_x * alpha_y - delta_y * alpha_x
    terms_list = [
        kernel_three * cross_x,
        kernel_three * cross_y,
        kernel_three * cross_z,
        kernel_three * alpha_x,
        kernel_three * alpha_y,
        kernel_three * alpha_z,
    ]
    for along in (delta_x, delta_y, delta_z):
        for cross in (cross_x, cross_y, cross_z):
            terms_list.append(kernel_five * along * cross)
    return jnp.stack([jnp.sum(term, axis=1) for term in terms_list])


def pair_kernel(source_ref, target_ref, out_ref):
    source_total = source_ref.shape[1]
    halves = 2 if target_ref.shape[1] % 16 == 0 else 1
    part = target_ref.shape[1] // halves
    target_x = [target_ref[0, k * part : (k + 1) * part] for k in range(halves)]
    target_y = [target_ref[1, k * part : (k + 1) * part] for k in range(halves)]
    target_z = [target_ref[2, k * part : (k + 1) * part] for k in range(halves)]

    def one_source(index, running):
        source_x = source_ref[0, index]
        source_y = source_ref[1, index]
        source_z = source_ref[2, index]
        alpha_x = source_ref[3, index]
        alpha_y = source_ref[4, index]
        alpha_z = source_ref[5, index]
        core_sq = source_ref[6, index]
        updated = []
        for k in range(halves):
            delta_x = target_x[k] - source_x
            delta_y = target_y[k] - source_y
            delta_z = target_z[k] - source_z
            radius_sq = delta_x * delta_x + delta_y * delta_y + delta_z * delta_z + core_sq
            inverse = lax.rsqrt(radius_sq)
            inverse_sq = inverse * inverse
            kernel_three = inverse_sq * inverse
            cross_x = delta_y * alpha_z - delta_z * alpha_y
            cross_y = delta_z * alpha_x - delta_x * alpha_z
            cross_z = delta_x * alpha_y - delta_y * alpha_x
            three_x = kernel_three * cross_x
            three_y = kernel_three * cross_y
            three_z = kernel_three * cross_z
            terms = [
                three_x,
                three_y,
                three_z,
                kernel_three * alpha_x,
                kernel_three * alpha_y,
                kernel_three * alpha_z,
            ]
            for along in (delta_x, delta_y, delta_z):
                scaled = inverse_sq * along
                terms.extend([scaled * three_x, scaled * three_y, scaled * three_z])
            terms = terms[:ROWS]
            mine = running[ROWS * k : ROWS * k + ROWS]
            updated.extend(total + term for total, term in zip(mine, terms))
        return tuple(updated)

    start = tuple(jnp.zeros_like(target_x[0]) for _ in range(ROWS * halves))
    running = lax.fori_loop(0, source_total, one_source, start, unroll=32)
    for k in range(halves):
        for row in range(ROWS):
            out_ref[row, k * part : (k + 1) * part] = running[ROWS * k + row]


def pair_sums(target_pos, source_pos, source_str, source_core):
    target_total = target_pos.shape[1]
    sublanes = target_total // 128
    tile = 16 if sublanes % 16 == 0 else sublanes
    sources = jnp.concatenate(
        [source_pos, source_str, source_core * source_core, jnp.zeros_like(source_core)], axis=0
    )
    targets = target_pos.reshape(3, sublanes, 128)
    sums = pl.pallas_call(
        pair_kernel,
        grid=(sublanes // tile,),
        in_specs=[
            pl.BlockSpec(memory_space=pltpu.SMEM),
            pl.BlockSpec((3, tile, 128), lambda step: (0, step, 0)),
        ],
        out_specs=pl.BlockSpec((ROWS, tile, 128), lambda step: (0, step, 0)),
        out_shape=jax.ShapeDtypeStruct((ROWS, sublanes, 128), jnp.float32),
    )(sources, targets)
    return sums.reshape(ROWS, target_total)


def combine_rows(kernel_sums):
    biot_scale = -1.0 / (4.0 * math.pi)
    swirl_x, swirl_y, swirl_z = (kernel_sums[3], kernel_sums[4], kernel_sums[5])
    zero_row = jnp.zeros_like(swirl_x)
    levi_terms = [
        [zero_row, swirl_z, -swirl_y],
        [-swirl_z, zero_row, swirl_x],
        [swirl_y, -swirl_x, zero_row],
    ]
    out_rows = [
        biot_scale * kernel_sums[0],
        biot_scale * kernel_sums[1],
        biot_scale * kernel_sums[2],
    ]
    for comp_m in range(3):
        for comp_n in range(3):
            out_rows.append(
                biot_scale
                * (levi_terms[comp_m][comp_n] - 3.0 * kernel_sums[6 + comp_n * 3 + comp_m])
            )
    return jnp.stack(out_rows)


def apply_mask(finished_rows, slot_counts, slot_cap):
    slot_ids = jnp.arange(slot_cap).astype(slot_counts.dtype)
    alive_mask = (slot_ids[None, :] < slot_counts[:, None]).astype(jnp.float32).reshape(-1)
    masked = finished_rows * alive_mask[None, :]
    cell_total = slot_counts.shape[0]
    return (
        masked[0:3].reshape(3, cell_total, slot_cap),
        masked[3:12].reshape(9, cell_total, slot_cap),
    )


def per_device(band_cells, cell_counts, cell_assign, wake_pos, wake_strength, wake_core):
    axes = ("row", "col")
    col_devs = lax.axis_size("col")
    cell_total = band_cells.shape[1]
    slot_cap = band_cells.shape[2]
    group_cells = cell_total * col_devs
    packed = jnp.concatenate(
        [
            band_cells.transpose(1, 0, 2).reshape(cell_total, 3 * slot_cap),
            cell_counts.astype(jnp.float32)[:, None],
            cell_assign.astype(jnp.float32)[:, None],
        ],
        axis=1,
    )
    devices = lax.axis_size("row") * col_devs
    copies = jnp.broadcast_to(packed[None], (devices,) + packed.shape)
    every_cell = lax.all_to_all(copies, axes, 0, 0, tiled=True)
    all_cells = devices * cell_total
    every_cell = every_cell.reshape(all_cells, packed.shape[1])
    groups = all_cells // group_cells
    grouped = every_cell.reshape(groups, group_cells, 3 * slot_cap + 2)
    within = grouped[:, :, -1].astype(jnp.int32) % group_cells
    position = jnp.arange(group_cells, dtype=jnp.int32)
    chosen = within[:, None, :] == position[None, :, None]
    relaid = jnp.sum(
        jnp.where(chosen[:, :, :, None], grouped[:, None, :, : 3 * slot_cap + 1], 0.0), axis=2
    ).reshape(all_cells, 3 * slot_cap + 1)
    target_pos = relaid[:, : 3 * slot_cap].reshape(all_cells, 3, slot_cap)
    target_pos = target_pos.transpose(1, 0, 2).reshape(3, all_cells * slot_cap)
    device = lax.axis_index("row") * col_devs + lax.axis_index("col")
    own_counts = lax.dynamic_slice_in_dim(relaid[:, 3 * slot_cap], device * cell_total, cell_total)
    local_sums = pair_sums(target_pos, wake_pos, wake_strength, wake_core)
    rows = local_sums.shape[0]
    by_device = local_sums.reshape(rows, devices, cell_total * slot_cap).transpose(1, 0, 2)
    own_rows = jnp.sum(lax.all_to_all(by_device, axes, 0, 0, tiled=True), axis=0)
    own_rows = jnp.concatenate([own_rows, -(own_rows[6:7] + own_rows[10:11])], axis=0)
    finished_rows = combine_rows(own_rows)
    return apply_mask(finished_rows, own_counts, slot_cap)


def solution(mesh):
    placed = (
        P(None, ("row", "col"), None),
        P(("row", "col")),
        P(("row", "col")),
        P(None, ("row", "col")),
        P(None, ("row", "col")),
        P(None, ("row", "col")),
    )
    return jax.shard_map(
        per_device,
        mesh=mesh,
        in_specs=placed,
        out_specs=(P(None, ("row", "col"), None), P(None, ("row", "col"), None)),
        check_vma=False,
    )
```

```python
import math

import jax
import jax.numpy as jnp
from jax import lax
from jax.experimental import pallas as pl
from jax.experimental.pallas import tpu as pltpu
from jax.sharding import PartitionSpec as P

HIGHEST = lax.Precision.HIGHEST
ROWS = 14


def block_sums(target_pos, source_pos, source_str, source_core):
    delta_x = target_pos[0][:, None] - source_pos[0][None, :]
    delta_y = target_pos[1][:, None] - source_pos[1][None, :]
    delta_z = target_pos[2][:, None] - source_pos[2][None, :]
    radius_sq = (
        delta_x * delta_x
        + delta_y * delta_y
        + delta_z * delta_z
        + source_core[0][None, :] * source_core[0][None, :]
    )
    inverse = lax.rsqrt(radius_sq)
    kernel_three = inverse * inverse * inverse
    kernel_five = kernel_three * inverse * inverse
    alpha_x = source_str[0][None, :]
    alpha_y = source_str[1][None, :]
    alpha_z = source_str[2][None, :]
    cross_x = delta_y * alpha_z - delta_z * alpha_y
    cross_y = delta_z * alpha_x - delta_x * alpha_z
    cross_z = delta_x * alpha_y - delta_y * alpha_x
    terms_list = [
        kernel_three * cross_x,
        kernel_three * cross_y,
        kernel_three * cross_z,
        kernel_three * alpha_x,
        kernel_three * alpha_y,
        kernel_three * alpha_z,
    ]
    for along in (delta_x, delta_y, delta_z):
        for cross in (cross_x, cross_y, cross_z):
            terms_list.append(kernel_five * along * cross)
    return jnp.stack([jnp.sum(term, axis=1) for term in terms_list])


def pair_kernel(source_ref, target_ref, out_ref):
    source_total = source_ref.shape[1]
    halves = 2 if target_ref.shape[1] % 16 == 0 else 1
    part = target_ref.shape[1] // halves
    target_x = [target_ref[0, k * part : (k + 1) * part] for k in range(halves)]
    target_y = [target_ref[1, k * part : (k + 1) * part] for k in range(halves)]
    target_z = [target_ref[2, k * part : (k + 1) * part] for k in range(halves)]

    def one_source(index, running):
        source_x = source_ref[0, index]
        source_y = source_ref[1, index]
        source_z = source_ref[2, index]
        alpha_x = source_ref[3, index]
        alpha_y = source_ref[4, index]
        alpha_z = source_ref[5, index]
        core_sq = source_ref[6, index]
        updated = []
        for k in range(halves):
            delta_x = target_x[k] - source_x
            delta_y = target_y[k] - source_y
            delta_z = target_z[k] - source_z
            radius_sq = delta_x * delta_x + delta_y * delta_y + delta_z * delta_z + core_sq
            inverse = lax.rsqrt(radius_sq)
            inverse_sq = inverse * inverse
            kernel_three = inverse_sq * inverse
            swirl_x = kernel_three * alpha_x
            swirl_y = kernel_three * alpha_y
            swirl_z = kernel_three * alpha_z
            three_x = delta_y * swirl_z - delta_z * swirl_y
            three_y = delta_z * swirl_x - delta_x * swirl_z
            three_z = delta_x * swirl_y - delta_y * swirl_x
            terms = [three_x, three_y, three_z, swirl_x, swirl_y, swirl_z]
            for along in (delta_x, delta_y, delta_z):
                scaled = inverse_sq * along
                terms.extend([scaled * three_x, scaled * three_y, scaled * three_z])
            terms = terms[:ROWS]
            mine = running[ROWS * k : ROWS * k + ROWS]
            updated.extend(total + term for total, term in zip(mine, terms))
        return tuple(updated)

    start = tuple(jnp.zeros_like(target_x[0]) for _ in range(ROWS * halves))
    running = lax.fori_loop(0, source_total, one_source, start, unroll=32)
    for k in range(halves):
        for row in range(ROWS):
            out_ref[row, k * part : (k + 1) * part] = running[ROWS * k + row]


def pair_sums(target_pos, source_pos, source_str, source_core):
    target_total = target_pos.shape[1]
    sublanes = target_total // 128
    tile = 16 if sublanes % 16 == 0 else sublanes
    sources = jnp.concatenate(
        [source_pos, source_str, source_core * source_core, jnp.zeros_like(source_core)], axis=0
    )
    targets = target_pos.reshape(3, sublanes, 128)
    sums = pl.pallas_call(
        pair_kernel,
        grid=(sublanes // tile,),
        in_specs=[
            pl.BlockSpec(memory_space=pltpu.SMEM),
            pl.BlockSpec((3, tile, 128), lambda step: (0, step, 0)),
        ],
        out_specs=pl.BlockSpec((ROWS, tile, 128), lambda step: (0, step, 0)),
        out_shape=jax.ShapeDtypeStruct((ROWS, sublanes, 128), jnp.float32),
    )(sources, targets)
    return sums.reshape(ROWS, target_total)


def combine_rows(kernel_sums):
    biot_scale = -1.0 / (4.0 * math.pi)
    swirl_x, swirl_y, swirl_z = (kernel_sums[3], kernel_sums[4], kernel_sums[5])
    zero_row = jnp.zeros_like(swirl_x)
    levi_terms = [
        [zero_row, swirl_z, -swirl_y],
        [-swirl_z, zero_row, swirl_x],
        [swirl_y, -swirl_x, zero_row],
    ]
    out_rows = [
        biot_scale * kernel_sums[0],
        biot_scale * kernel_sums[1],
        biot_scale * kernel_sums[2],
    ]
    for comp_m in range(3):
        for comp_n in range(3):
            out_rows.append(
                biot_scale
                * (levi_terms[comp_m][comp_n] - 3.0 * kernel_sums[6 + comp_n * 3 + comp_m])
            )
    return jnp.stack(out_rows)


def apply_mask(finished_rows, slot_counts, slot_cap):
    slot_ids = jnp.arange(slot_cap).astype(slot_counts.dtype)
    alive_mask = (slot_ids[None, :] < slot_counts[:, None]).astype(jnp.float32).reshape(-1)
    masked = finished_rows * alive_mask[None, :]
    cell_total = slot_counts.shape[0]
    return (
        masked[0:3].reshape(3, cell_total, slot_cap),
        masked[3:12].reshape(9, cell_total, slot_cap),
    )


def per_device(band_cells, cell_counts, cell_assign, wake_pos, wake_strength, wake_core):
    axes = ("row", "col")
    col_devs = lax.axis_size("col")
    cell_total = band_cells.shape[1]
    slot_cap = band_cells.shape[2]
    group_cells = cell_total * col_devs
    packed = jnp.concatenate(
        [
            band_cells.transpose(1, 0, 2).reshape(cell_total, 3 * slot_cap),
            cell_counts.astype(jnp.float32)[:, None],
            cell_assign.astype(jnp.float32)[:, None],
        ],
        axis=1,
    )
    devices = lax.axis_size("row") * col_devs
    copies = jnp.broadcast_to(packed[None], (devices,) + packed.shape)
    every_cell = lax.all_to_all(copies, axes, 0, 0, tiled=True)
    all_cells = devices * cell_total
    every_cell = every_cell.reshape(all_cells, packed.shape[1])
    groups = all_cells // group_cells
    grouped = every_cell.reshape(groups, group_cells, 3 * slot_cap + 2)
    within = grouped[:, :, -1].astype(jnp.int32) % group_cells
    position = jnp.arange(group_cells, dtype=jnp.int32)
    chosen = within[:, None, :] == position[None, :, None]
    relaid = jnp.sum(
        jnp.where(chosen[:, :, :, None], grouped[:, None, :, : 3 * slot_cap + 1], 0.0), axis=2
    ).reshape(all_cells, 3 * slot_cap + 1)
    target_pos = relaid[:, : 3 * slot_cap].reshape(all_cells, 3, slot_cap)
    target_pos = target_pos.transpose(1, 0, 2).reshape(3, all_cells * slot_cap)
    device = lax.axis_index("row") * col_devs + lax.axis_index("col")
    own_counts = lax.dynamic_slice_in_dim(relaid[:, 3 * slot_cap], device * cell_total, cell_total)
    local_sums = pair_sums(target_pos, wake_pos, wake_strength, wake_core)
    rows = local_sums.shape[0]
    by_device = local_sums.reshape(rows, devices, cell_total * slot_cap).transpose(1, 0, 2)
    own_rows = jnp.sum(lax.all_to_all(by_device, axes, 0, 0, tiled=True), axis=0)
    own_rows = jnp.concatenate([own_rows, -(own_rows[6:7] + own_rows[10:11])], axis=0)
    finished_rows = combine_rows(own_rows)
    return apply_mask(finished_rows, own_counts, slot_cap)


def solution(mesh):
    placed = (
        P(None, ("row", "col"), None),
        P(("row", "col")),
        P(("row", "col")),
        P(None, ("row", "col")),
        P(None, ("row", "col")),
        P(None, ("row", "col")),
    )
    return jax.shard_map(
        per_device,
        mesh=mesh,
        in_specs=placed,
        out_specs=(P(None, ("row", "col"), None), P(None, ("row", "col"), None)),
        check_vma=False,
    )
```

```python
import math

import jax
import jax.numpy as jnp
from jax import lax
from jax.experimental import pallas as pl
from jax.experimental.pallas import tpu as pltpu
from jax.sharding import PartitionSpec as P

HIGHEST = lax.Precision.HIGHEST
ROWS = 14


def block_sums(target_pos, source_pos, source_str, source_core):
    delta_x = target_pos[0][:, None] - source_pos[0][None, :]
    delta_y = target_pos[1][:, None] - source_pos[1][None, :]
    delta_z = target_pos[2][:, None] - source_pos[2][None, :]
    radius_sq = (
        delta_x * delta_x
        + delta_y * delta_y
        + delta_z * delta_z
        + source_core[0][None, :] * source_core[0][None, :]
    )
    inverse = lax.rsqrt(radius_sq)
    kernel_three = inverse * inverse * inverse
    kernel_five = kernel_three * inverse * inverse
    alpha_x = source_str[0][None, :]
    alpha_y = source_str[1][None, :]
    alpha_z = source_str[2][None, :]
    cross_x = delta_y * alpha_z - delta_z * alpha_y
    cross_y = delta_z * alpha_x - delta_x * alpha_z
    cross_z = delta_x * alpha_y - delta_y * alpha_x
    terms_list = [
        kernel_three * cross_x,
        kernel_three * cross_y,
        kernel_three * cross_z,
        kernel_three * alpha_x,
        kernel_three * alpha_y,
        kernel_three * alpha_z,
    ]
    for along in (delta_x, delta_y, delta_z):
        for cross in (cross_x, cross_y, cross_z):
            terms_list.append(kernel_five * along * cross)
    return jnp.stack([jnp.sum(term, axis=1) for term in terms_list])


def pair_kernel(source_ref, target_ref, out_ref):
    source_total = source_ref.shape[1]
    halves = 2 if target_ref.shape[1] % 16 == 0 else 1
    part = target_ref.shape[1] // halves
    target_x = [target_ref[0, k * part : (k + 1) * part] for k in range(halves)]
    target_y = [target_ref[1, k * part : (k + 1) * part] for k in range(halves)]
    target_z = [target_ref[2, k * part : (k + 1) * part] for k in range(halves)]

    def one_source(index, running):
        source_x = source_ref[0, index]
        source_y = source_ref[1, index]
        source_z = source_ref[2, index]
        alpha_x = source_ref[3, index]
        alpha_y = source_ref[4, index]
        alpha_z = source_ref[5, index]
        core_sq = source_ref[6, index]
        updated = []
        for k in range(halves):
            delta_x = target_x[k] - source_x
            delta_y = target_y[k] - source_y
            delta_z = target_z[k] - source_z
            radius_sq = delta_x * delta_x + delta_y * delta_y + delta_z * delta_z + core_sq
            inverse = lax.rsqrt(radius_sq)
            inverse_sq = inverse * inverse
            kernel_three = inverse_sq * inverse
            swirl_x = kernel_three * alpha_x
            swirl_y = kernel_three * alpha_y
            swirl_z = kernel_three * alpha_z
            three_x = delta_y * swirl_z - delta_z * swirl_y
            three_y = delta_z * swirl_x - delta_x * swirl_z
            three_z = delta_x * swirl_y - delta_y * swirl_x
            terms = [three_x, three_y, three_z, swirl_x, swirl_y, swirl_z]
            for along in (delta_x, delta_y, delta_z):
                scaled = inverse_sq * along
                terms.extend([scaled * three_x, scaled * three_y, scaled * three_z])
            terms = terms[:ROWS]
            mine = running[ROWS * k : ROWS * k + ROWS]
            updated.extend(total + term for total, term in zip(mine, terms))
        return tuple(updated)

    start = tuple(jnp.zeros_like(target_x[0]) for _ in range(ROWS * halves))
    running = lax.fori_loop(0, source_total, one_source, start, unroll=32)
    for k in range(halves):
        for row in range(ROWS):
            out_ref[row, k * part : (k + 1) * part] = running[ROWS * k + row]


def pair_sums(target_pos, source_pos, source_str, source_core):
    target_total = target_pos.shape[1]
    sublanes = target_total // 128
    tile = 16 if sublanes % 16 == 0 else sublanes
    sources = jnp.concatenate(
        [source_pos, source_str, source_core * source_core, jnp.zeros_like(source_core)], axis=0
    )
    targets = target_pos.reshape(3, sublanes, 128)
    sums = pl.pallas_call(
        pair_kernel,
        grid=(sublanes // tile,),
        in_specs=[
            pl.BlockSpec(memory_space=pltpu.SMEM),
            pl.BlockSpec((3, tile, 128), lambda step: (0, step, 0)),
        ],
        out_specs=pl.BlockSpec((ROWS, tile, 128), lambda step: (0, step, 0)),
        out_shape=jax.ShapeDtypeStruct((ROWS, sublanes, 128), jnp.float32),
    )(sources, targets)
    return sums.reshape(ROWS, target_total)


def combine_rows(kernel_sums):
    biot_scale = -1.0 / (4.0 * math.pi)
    swirl_x, swirl_y, swirl_z = (kernel_sums[3], kernel_sums[4], kernel_sums[5])
    zero_row = jnp.zeros_like(swirl_x)
    levi_terms = [
        [zero_row, swirl_z, -swirl_y],
        [-swirl_z, zero_row, swirl_x],
        [swirl_y, -swirl_x, zero_row],
    ]
    out_rows = [
        biot_scale * kernel_sums[0],
        biot_scale * kernel_sums[1],
        biot_scale * kernel_sums[2],
    ]
    for comp_m in range(3):
        for comp_n in range(3):
            out_rows.append(
                biot_scale
                * (levi_terms[comp_m][comp_n] - 3.0 * kernel_sums[6 + comp_n * 3 + comp_m])
            )
    return jnp.stack(out_rows)


def apply_mask(finished_rows, slot_counts, slot_cap):
    slot_ids = jnp.arange(slot_cap).astype(slot_counts.dtype)
    alive_mask = (slot_ids[None, :] < slot_counts[:, None]).astype(jnp.float32).reshape(-1)
    masked = finished_rows * alive_mask[None, :]
    cell_total = slot_counts.shape[0]
    return (
        masked[0:3].reshape(3, cell_total, slot_cap),
        masked[3:12].reshape(9, cell_total, slot_cap),
    )


def per_device(band_cells, cell_counts, cell_assign, wake_pos, wake_strength, wake_core):
    axes = ("row", "col")
    col_devs = lax.axis_size("col")
    cell_total = band_cells.shape[1]
    slot_cap = band_cells.shape[2]
    group_cells = cell_total * col_devs
    packed = jnp.concatenate(
        [
            band_cells.transpose(1, 0, 2).reshape(cell_total, 3 * slot_cap),
            cell_counts.astype(jnp.float32)[:, None],
            cell_assign.astype(jnp.float32)[:, None],
        ],
        axis=1,
    )
    devices = lax.axis_size("row") * col_devs
    flat = packed.reshape(1, 1, packed.size)
    copies = jnp.broadcast_to(flat, (devices, 1, packed.size))
    every_cell = lax.all_to_all(copies, axes, 0, 0, tiled=True)
    all_cells = devices * cell_total
    every_cell = every_cell.reshape(all_cells, packed.shape[1])
    groups = all_cells // group_cells
    grouped = every_cell.reshape(groups, group_cells, 3 * slot_cap + 2)
    within = grouped[:, :, -1].astype(jnp.int32) % group_cells
    position = jnp.arange(group_cells, dtype=jnp.int32)
    chosen = within[:, None, :] == position[None, :, None]
    relaid = jnp.sum(
        jnp.where(chosen[:, :, :, None], grouped[:, None, :, : 3 * slot_cap + 1], 0.0), axis=2
    ).reshape(all_cells, 3 * slot_cap + 1)
    target_pos = relaid[:, : 3 * slot_cap].reshape(all_cells, 3, slot_cap)
    target_pos = target_pos.transpose(1, 0, 2).reshape(3, all_cells * slot_cap)
    device = lax.axis_index("row") * col_devs + lax.axis_index("col")
    own_counts = lax.dynamic_slice_in_dim(relaid[:, 3 * slot_cap], device * cell_total, cell_total)
    local_sums = pair_sums(target_pos, wake_pos, wake_strength, wake_core)
    rows = local_sums.shape[0]
    by_device = local_sums.reshape(rows, devices, cell_total * slot_cap).transpose(1, 0, 2)
    own_rows = jnp.sum(lax.all_to_all(by_device, axes, 0, 0, tiled=True), axis=0)
    own_rows = jnp.concatenate([own_rows, -(own_rows[6:7] + own_rows[10:11])], axis=0)
    finished_rows = combine_rows(own_rows)
    return apply_mask(finished_rows, own_counts, slot_cap)


def solution(mesh):
    placed = (
        P(None, ("row", "col"), None),
        P(("row", "col")),
        P(("row", "col")),
        P(None, ("row", "col")),
        P(None, ("row", "col")),
        P(None, ("row", "col")),
    )
    return jax.shard_map(
        per_device,
        mesh=mesh,
        in_specs=placed,
        out_specs=(P(None, ("row", "col"), None), P(None, ("row", "col"), None)),
        check_vma=False,
    )
```

```python
import math

import jax
import jax.numpy as jnp
from jax import lax
from jax.experimental import pallas as pl
from jax.experimental.pallas import tpu as pltpu
from jax.sharding import PartitionSpec as P

HIGHEST = lax.Precision.HIGHEST
ROWS = 14


def block_sums(target_pos, source_pos, source_str, source_core):
    delta_x = target_pos[0][:, None] - source_pos[0][None, :]
    delta_y = target_pos[1][:, None] - source_pos[1][None, :]
    delta_z = target_pos[2][:, None] - source_pos[2][None, :]
    radius_sq = (
        delta_x * delta_x
        + delta_y * delta_y
        + delta_z * delta_z
        + source_core[0][None, :] * source_core[0][None, :]
    )
    inverse = lax.rsqrt(radius_sq)
    kernel_three = inverse * inverse * inverse
    kernel_five = kernel_three * inverse * inverse
    alpha_x = source_str[0][None, :]
    alpha_y = source_str[1][None, :]
    alpha_z = source_str[2][None, :]
    cross_x = delta_y * alpha_z - delta_z * alpha_y
    cross_y = delta_z * alpha_x - delta_x * alpha_z
    cross_z = delta_x * alpha_y - delta_y * alpha_x
    terms_list = [
        kernel_three * cross_x,
        kernel_three * cross_y,
        kernel_three * cross_z,
        kernel_three * alpha_x,
        kernel_three * alpha_y,
        kernel_three * alpha_z,
    ]
    for along in (delta_x, delta_y, delta_z):
        for cross in (cross_x, cross_y, cross_z):
            terms_list.append(kernel_five * along * cross)
    return jnp.stack([jnp.sum(term, axis=1) for term in terms_list])


def pair_kernel(source_ref, target_ref, out_ref):
    source_total = source_ref.shape[1]
    halves = 1
    part = target_ref.shape[1] // halves
    target_x = [target_ref[0, k * part : (k + 1) * part] for k in range(halves)]
    target_y = [target_ref[1, k * part : (k + 1) * part] for k in range(halves)]
    target_z = [target_ref[2, k * part : (k + 1) * part] for k in range(halves)]

    def one_source(index, running):
        source_x = source_ref[0, index]
        source_y = source_ref[1, index]
        source_z = source_ref[2, index]
        alpha_x = source_ref[3, index]
        alpha_y = source_ref[4, index]
        alpha_z = source_ref[5, index]
        core_sq = source_ref[6, index]
        updated = []
        for k in range(halves):
            delta_x = target_x[k] - source_x
            delta_y = target_y[k] - source_y
            delta_z = target_z[k] - source_z
            radius_sq = delta_x * delta_x + delta_y * delta_y + delta_z * delta_z + core_sq
            inverse = lax.rsqrt(radius_sq)
            inverse_sq = inverse * inverse
            kernel_three = inverse_sq * inverse
            swirl_x = kernel_three * alpha_x
            swirl_y = kernel_three * alpha_y
            swirl_z = kernel_three * alpha_z
            three_x = delta_y * swirl_z - delta_z * swirl_y
            three_y = delta_z * swirl_x - delta_x * swirl_z
            three_z = delta_x * swirl_y - delta_y * swirl_x
            terms = [three_x, three_y, three_z, swirl_x, swirl_y, swirl_z]
            for along in (delta_x, delta_y, delta_z):
                scaled = inverse_sq * along
                terms.extend([scaled * three_x, scaled * three_y, scaled * three_z])
            terms = terms[:ROWS]
            mine = running[ROWS * k : ROWS * k + ROWS]
            updated.extend(total + term for total, term in zip(mine, terms))
        return tuple(updated)

    start = tuple(jnp.zeros_like(target_x[0]) for _ in range(ROWS * halves))
    running = lax.fori_loop(0, source_total, one_source, start, unroll=32)
    for k in range(halves):
        for row in range(ROWS):
            out_ref[row, k * part : (k + 1) * part] = running[ROWS * k + row]


def pair_sums(target_pos, source_pos, source_str, source_core):
    target_total = target_pos.shape[1]
    sublanes = target_total // 128
    tile = 16 if sublanes % 16 == 0 else sublanes
    sources = jnp.concatenate(
        [source_pos, source_str, source_core * source_core, jnp.zeros_like(source_core)], axis=0
    )
    targets = target_pos.reshape(3, sublanes, 128)
    sums = pl.pallas_call(
        pair_kernel,
        grid=(sublanes // tile,),
        in_specs=[
            pl.BlockSpec(memory_space=pltpu.SMEM),
            pl.BlockSpec((3, tile, 128), lambda step: (0, step, 0)),
        ],
        out_specs=pl.BlockSpec((ROWS, tile, 128), lambda step: (0, step, 0)),
        out_shape=jax.ShapeDtypeStruct((ROWS, sublanes, 128), jnp.float32),
    )(sources, targets)
    return sums.reshape(ROWS, target_total)


def combine_rows(kernel_sums):
    biot_scale = -1.0 / (4.0 * math.pi)
    swirl_x, swirl_y, swirl_z = (kernel_sums[3], kernel_sums[4], kernel_sums[5])
    zero_row = jnp.zeros_like(swirl_x)
    levi_terms = [
        [zero_row, swirl_z, -swirl_y],
        [-swirl_z, zero_row, swirl_x],
        [swirl_y, -swirl_x, zero_row],
    ]
    out_rows = [
        biot_scale * kernel_sums[0],
        biot_scale * kernel_sums[1],
        biot_scale * kernel_sums[2],
    ]
    for comp_m in range(3):
        for comp_n in range(3):
            out_rows.append(
                biot_scale
                * (levi_terms[comp_m][comp_n] - 3.0 * kernel_sums[6 + comp_n * 3 + comp_m])
            )
    return jnp.stack(out_rows)


def apply_mask(finished_rows, slot_counts, slot_cap):
    slot_ids = jnp.arange(slot_cap).astype(slot_counts.dtype)
    alive_mask = (slot_ids[None, :] < slot_counts[:, None]).astype(jnp.float32).reshape(-1)
    masked = finished_rows * alive_mask[None, :]
    cell_total = slot_counts.shape[0]
    return (
        masked[0:3].reshape(3, cell_total, slot_cap),
        masked[3:12].reshape(9, cell_total, slot_cap),
    )


def per_device(band_cells, cell_counts, cell_assign, wake_pos, wake_strength, wake_core):
    axes = ("row", "col")
    col_devs = lax.axis_size("col")
    cell_total = band_cells.shape[1]
    slot_cap = band_cells.shape[2]
    group_cells = cell_total * col_devs
    packed = jnp.concatenate(
        [
            band_cells.transpose(1, 0, 2).reshape(cell_total, 3 * slot_cap),
            cell_counts.astype(jnp.float32)[:, None],
            cell_assign.astype(jnp.float32)[:, None],
        ],
        axis=1,
    )
    devices = lax.axis_size("row") * col_devs
    flat = packed.reshape(1, 1, packed.size)
    copies = jnp.broadcast_to(flat, (devices, 1, packed.size))
    every_cell = lax.all_to_all(copies, axes, 0, 0, tiled=True)
    all_cells = devices * cell_total
    every_cell = every_cell.reshape(all_cells, packed.shape[1])
    groups = all_cells // group_cells
    grouped = every_cell.reshape(groups, group_cells, 3 * slot_cap + 2)
    within = grouped[:, :, -1].astype(jnp.int32) % group_cells
    lane = jnp.arange(group_cells * slot_cap, dtype=jnp.int32)
    chosen = within[:, None, :] == (lane // slot_cap)[None, :, None]
    coords = grouped[:, :, : 3 * slot_cap].reshape(groups, group_cells, 3, slot_cap)
    picked = coords[..., 0][..., None]
    for slot in range(1, slot_cap):
        picked = jnp.where((lane % slot_cap) == slot, coords[..., slot][..., None], picked)
    picked = picked.transpose(2, 0, 3, 1)
    target_pos = jnp.sum(jnp.where(chosen[None], picked, 0.0), axis=-1)
    target_pos = target_pos.reshape(3, all_cells * slot_cap)
    device = lax.axis_index("row") * col_devs + lax.axis_index("col")
    own_group = lax.dynamic_index_in_dim(grouped, device // col_devs, 0, keepdims=False)
    own_within = lax.dynamic_index_in_dim(within, device // col_devs, 0, keepdims=False)
    own_slots = (device % col_devs) * cell_total + jnp.arange(cell_total, dtype=jnp.int32)
    own_counts = jnp.sum(
        jnp.where(own_within[None, :] == own_slots[:, None], own_group[None, :, 3 * slot_cap], 0.0),
        axis=1,
    )
    local_sums = pair_sums(target_pos, wake_pos, wake_strength, wake_core)
    rows = local_sums.shape[0]
    by_device = local_sums.reshape(rows, devices, cell_total * slot_cap).transpose(1, 0, 2)
    own_rows = jnp.sum(lax.all_to_all(by_device, axes, 0, 0, tiled=True), axis=0)
    own_rows = jnp.concatenate([own_rows, -(own_rows[6:7] + own_rows[10:11])], axis=0)
    finished_rows = combine_rows(own_rows)
    return apply_mask(finished_rows, own_counts, slot_cap)


def solution(mesh):
    placed = (
        P(None, ("row", "col"), None),
        P(("row", "col")),
        P(("row", "col")),
        P(None, ("row", "col")),
        P(None, ("row", "col")),
        P(None, ("row", "col")),
    )
    return jax.shard_map(
        per_device,
        mesh=mesh,
        in_specs=placed,
        out_specs=(P(None, ("row", "col"), None), P(None, ("row", "col"), None)),
        check_vma=False,
    )
```

```python
import math

import jax
import jax.numpy as jnp
from jax import lax
from jax.experimental import pallas as pl
from jax.experimental.pallas import tpu as pltpu
from jax.sharding import PartitionSpec as P

HIGHEST = lax.Precision.HIGHEST
ROWS = 14


def block_sums(target_pos, source_pos, source_str, source_core):
    delta_x = target_pos[0][:, None] - source_pos[0][None, :]
    delta_y = target_pos[1][:, None] - source_pos[1][None, :]
    delta_z = target_pos[2][:, None] - source_pos[2][None, :]
    radius_sq = (
        delta_x * delta_x
        + delta_y * delta_y
        + delta_z * delta_z
        + source_core[0][None, :] * source_core[0][None, :]
    )
    inverse = lax.rsqrt(radius_sq)
    kernel_three = inverse * inverse * inverse
    kernel_five = kernel_three * inverse * inverse
    alpha_x = source_str[0][None, :]
    alpha_y = source_str[1][None, :]
    alpha_z = source_str[2][None, :]
    cross_x = delta_y * alpha_z - delta_z * alpha_y
    cross_y = delta_z * alpha_x - delta_x * alpha_z
    cross_z = delta_x * alpha_y - delta_y * alpha_x
    terms_list = [
        kernel_three * cross_x,
        kernel_three * cross_y,
        kernel_three * cross_z,
        kernel_three * alpha_x,
        kernel_three * alpha_y,
        kernel_three * alpha_z,
    ]
    for along in (delta_x, delta_y, delta_z):
        for cross in (cross_x, cross_y, cross_z):
            terms_list.append(kernel_five * along * cross)
    return jnp.stack([jnp.sum(term, axis=1) for term in terms_list])


def pair_kernel(source_ref, target_ref, out_ref):
    chunk = source_ref.shape[1]
    shape = target_ref.shape[1:]
    target_x = target_ref[0]
    target_y = target_ref[1]
    target_z = target_ref[2]

    @pl.when(pl.program_id(0) == 0)
    def _():
        out_ref[...] = jnp.zeros_like(out_ref)

    def one_source(index, running):
        def spread(row):
            return jnp.broadcast_to(source_ref[row, pl.ds(index, 1), :], shape)

        delta_x = target_x - spread(0)
        delta_y = target_y - spread(1)
        delta_z = target_z - spread(2)
        alpha_x = spread(3)
        alpha_y = spread(4)
        alpha_z = spread(5)
        radius_sq = delta_x * delta_x + delta_y * delta_y + delta_z * delta_z + spread(6)
        inverse = lax.rsqrt(radius_sq)
        inverse_sq = inverse * inverse
        kernel_three = inverse_sq * inverse
        swirl_x = kernel_three * alpha_x
        swirl_y = kernel_three * alpha_y
        swirl_z = kernel_three * alpha_z
        three_x = delta_y * swirl_z - delta_z * swirl_y
        three_y = delta_z * swirl_x - delta_x * swirl_z
        three_z = delta_x * swirl_y - delta_y * swirl_x
        terms = [three_x, three_y, three_z, swirl_x, swirl_y, swirl_z]
        for along in (delta_x, delta_y, delta_z):
            scaled = inverse_sq * along
            terms.extend([scaled * three_x, scaled * three_y, scaled * three_z])
        return tuple(total + term for total, term in zip(running, terms[:ROWS]))

    start = tuple(out_ref[row] for row in range(ROWS))
    running = lax.fori_loop(0, chunk, one_source, start, unroll=32)
    for row in range(ROWS):
        out_ref[row] = running[row]


def spread_sources(source_pos, source_str, source_core):
    sources = jnp.concatenate([source_pos, source_str, source_core * source_core], axis=0)
    return jnp.broadcast_to(sources[:, :, None], sources.shape + (128,))


def pair_sums(target_pos, sources):
    target_total = target_pos.shape[1]
    source_total = sources.shape[1]
    sublanes = target_total // 128
    chunk = math.gcd(source_total, 1024)
    targets = target_pos.reshape(3, sublanes, 128)
    sums = pl.pallas_call(
        pair_kernel,
        grid=(source_total // chunk,),
        in_specs=[
            pl.BlockSpec((7, chunk, 128), lambda step: (0, step, 0)),
            pl.BlockSpec((3, sublanes, 128), lambda step: (0, 0, 0)),
        ],
        out_specs=pl.BlockSpec((ROWS, sublanes, 128), lambda step: (0, 0, 0)),
        out_shape=jax.ShapeDtypeStruct((ROWS, sublanes, 128), jnp.float32),
    )(sources, targets)
    return sums.reshape(ROWS, target_total)


def combine_rows(kernel_sums):
    biot_scale = -1.0 / (4.0 * math.pi)
    swirl_x, swirl_y, swirl_z = (kernel_sums[3], kernel_sums[4], kernel_sums[5])
    zero_row = jnp.zeros_like(swirl_x)
    levi_terms = [
        [zero_row, swirl_z, -swirl_y],
        [-swirl_z, zero_row, swirl_x],
        [swirl_y, -swirl_x, zero_row],
    ]
    out_rows = [
        biot_scale * kernel_sums[0],
        biot_scale * kernel_sums[1],
        biot_scale * kernel_sums[2],
    ]
    for comp_m in range(3):
        for comp_n in range(3):
            out_rows.append(
                biot_scale
                * (levi_terms[comp_m][comp_n] - 3.0 * kernel_sums[6 + comp_n * 3 + comp_m])
            )
    return jnp.stack(out_rows)


def apply_mask(finished_rows, slot_counts, slot_cap):
    slot_ids = jnp.arange(slot_cap).astype(slot_counts.dtype)
    alive_mask = (slot_ids[None, :] < slot_counts[:, None]).astype(jnp.float32).reshape(-1)
    masked = finished_rows * alive_mask[None, :]
    cell_total = slot_counts.shape[0]
    return (
        masked[0:3].reshape(3, cell_total, slot_cap),
        masked[3:12].reshape(9, cell_total, slot_cap),
    )


def per_device(band_cells, cell_counts, cell_assign, wake_pos, wake_strength, wake_core):
    axes = ("row", "col")
    col_devs = lax.axis_size("col")
    cell_total = band_cells.shape[1]
    slot_cap = band_cells.shape[2]
    group_cells = cell_total * col_devs
    packed = jnp.concatenate(
        [
            band_cells.transpose(1, 0, 2).reshape(cell_total, 3 * slot_cap),
            cell_counts.astype(jnp.float32)[:, None],
            cell_assign.astype(jnp.float32)[:, None],
        ],
        axis=1,
    )
    devices = lax.axis_size("row") * col_devs
    flat = packed.reshape(1, 1, packed.size)
    copies = jnp.broadcast_to(flat, (devices, 1, packed.size))
    sources = spread_sources(wake_pos, wake_strength, wake_core)
    copies, sources = lax.optimization_barrier((copies, sources))
    every_cell = lax.all_to_all(copies, axes, 0, 0, tiled=True)
    all_cells = devices * cell_total
    every_cell = every_cell.reshape(all_cells, packed.shape[1])
    groups = all_cells // group_cells
    grouped = every_cell.reshape(groups, group_cells, 3 * slot_cap + 2)
    within = grouped[:, :, -1].astype(jnp.int32) % group_cells
    lane = jnp.arange(group_cells * slot_cap, dtype=jnp.int32)
    chosen = within[:, None, :] == (lane // slot_cap)[None, :, None]
    coords = grouped[:, :, : 3 * slot_cap].reshape(groups, group_cells, 3, slot_cap)
    picked = coords[..., 0][..., None]
    for slot in range(1, slot_cap):
        picked = jnp.where((lane % slot_cap) == slot, coords[..., slot][..., None], picked)
    picked = picked.transpose(2, 0, 3, 1)
    target_pos = jnp.sum(jnp.where(chosen[None], picked, 0.0), axis=-1)
    target_pos = target_pos.reshape(3, all_cells * slot_cap)
    device = lax.axis_index("row") * col_devs + lax.axis_index("col")
    own_group = lax.dynamic_index_in_dim(grouped, device // col_devs, 0, keepdims=False)
    own_within = lax.dynamic_index_in_dim(within, device // col_devs, 0, keepdims=False)
    own_slots = (device % col_devs) * cell_total + jnp.arange(cell_total, dtype=jnp.int32)
    own_counts = jnp.sum(
        jnp.where(own_within[None, :] == own_slots[:, None], own_group[None, :, 3 * slot_cap], 0.0),
        axis=1,
    )
    local_sums = pair_sums(target_pos, sources)
    rows = local_sums.shape[0]
    by_device = local_sums.reshape(rows, devices, cell_total * slot_cap).transpose(1, 0, 2)
    own_rows = jnp.sum(lax.all_to_all(by_device, axes, 0, 0, tiled=True), axis=0)
    own_rows = jnp.concatenate([own_rows, -(own_rows[6:7] + own_rows[10:11])], axis=0)
    finished_rows = combine_rows(own_rows)
    return apply_mask(finished_rows, own_counts, slot_cap)


def solution(mesh):
    placed = (
        P(None, ("row", "col"), None),
        P(("row", "col")),
        P(("row", "col")),
        P(None, ("row", "col")),
        P(None, ("row", "col")),
        P(None, ("row", "col")),
    )
    return jax.shard_map(
        per_device,
        mesh=mesh,
        in_specs=placed,
        out_specs=(P(None, ("row", "col"), None), P(None, ("row", "col"), None)),
        check_vma=False,
    )
```

```python
import math

import jax
import jax.numpy as jnp
from jax import lax
from jax.experimental import pallas as pl
from jax.experimental.pallas import tpu as pltpu
from jax.sharding import PartitionSpec as P

HIGHEST = lax.Precision.HIGHEST
ROWS = 14


def block_sums(target_pos, source_pos, source_str, source_core):
    delta_x = target_pos[0][:, None] - source_pos[0][None, :]
    delta_y = target_pos[1][:, None] - source_pos[1][None, :]
    delta_z = target_pos[2][:, None] - source_pos[2][None, :]
    radius_sq = (
        delta_x * delta_x
        + delta_y * delta_y
        + delta_z * delta_z
        + source_core[0][None, :] * source_core[0][None, :]
    )
    inverse = lax.rsqrt(radius_sq)
    kernel_three = inverse * inverse * inverse
    kernel_five = kernel_three * inverse * inverse
    alpha_x = source_str[0][None, :]
    alpha_y = source_str[1][None, :]
    alpha_z = source_str[2][None, :]
    cross_x = delta_y * alpha_z - delta_z * alpha_y
    cross_y = delta_z * alpha_x - delta_x * alpha_z
    cross_z = delta_x * alpha_y - delta_y * alpha_x
    terms_list = [
        kernel_three * cross_x,
        kernel_three * cross_y,
        kernel_three * cross_z,
        kernel_three * alpha_x,
        kernel_three * alpha_y,
        kernel_three * alpha_z,
    ]
    for along in (delta_x, delta_y, delta_z):
        for cross in (cross_x, cross_y, cross_z):
            terms_list.append(kernel_five * along * cross)
    return jnp.stack([jnp.sum(term, axis=1) for term in terms_list])


def pair_kernel(source_ref, target_ref, out_ref):
    chunk = source_ref.shape[1]
    shape = target_ref.shape[1:]
    target_x = target_ref[0]
    target_y = target_ref[1]
    target_z = target_ref[2]

    @pl.when(pl.program_id(0) == 0)
    def _():
        out_ref[...] = jnp.zeros_like(out_ref)

    def one_source(index, running):
        def spread(row):
            return jnp.broadcast_to(source_ref[row, pl.ds(index, 1), :], shape)

        delta_x = target_x - spread(0)
        delta_y = target_y - spread(1)
        delta_z = target_z - spread(2)
        alpha_x = spread(3)
        alpha_y = spread(4)
        alpha_z = spread(5)
        radius_sq = delta_x * delta_x + delta_y * delta_y + delta_z * delta_z + spread(6)
        inverse = lax.rsqrt(radius_sq)
        inverse_sq = inverse * inverse
        kernel_three = inverse_sq * inverse
        swirl_x = kernel_three * alpha_x
        swirl_y = kernel_three * alpha_y
        swirl_z = kernel_three * alpha_z
        three_x = delta_y * swirl_z - delta_z * swirl_y
        three_y = delta_z * swirl_x - delta_x * swirl_z
        three_z = delta_x * swirl_y - delta_y * swirl_x
        terms = [three_x, three_y, three_z, swirl_x, swirl_y, swirl_z]
        for along in (delta_x, delta_y, delta_z):
            scaled = inverse_sq * along
            terms.extend([scaled * three_x, scaled * three_y, scaled * three_z])
        return tuple(total + term for total, term in zip(running, terms[:ROWS]))

    start = tuple(out_ref[row] for row in range(ROWS))
    running = lax.fori_loop(0, chunk, one_source, start, unroll=32)
    for row in range(ROWS):
        out_ref[row] = running[row]


def spread_sources(source_pos, source_str, source_core):
    sources = jnp.concatenate([source_pos, source_str, source_core * source_core], axis=0)
    return jnp.broadcast_to(sources[:, :, None], sources.shape + (128,))


def pair_sums(target_pos, sources):
    target_total = target_pos.shape[1]
    source_total = sources.shape[1]
    sublanes = target_total // 128
    chunk = math.gcd(source_total, 1024)
    targets = target_pos.reshape(3, sublanes, 128)
    sums = pl.pallas_call(
        pair_kernel,
        grid=(source_total // chunk,),
        in_specs=[
            pl.BlockSpec((7, chunk, 128), lambda step: (0, step, 0)),
            pl.BlockSpec((3, sublanes, 128), lambda step: (0, 0, 0)),
        ],
        out_specs=pl.BlockSpec((ROWS, sublanes, 128), lambda step: (0, 0, 0)),
        out_shape=jax.ShapeDtypeStruct((ROWS, sublanes, 128), jnp.float32),
    )(sources, targets)
    return sums.reshape(ROWS, target_total)


def combine_rows(kernel_sums):
    biot_scale = -1.0 / (4.0 * math.pi)
    swirl_x, swirl_y, swirl_z = (kernel_sums[3], kernel_sums[4], kernel_sums[5])
    zero_row = jnp.zeros_like(swirl_x)
    levi_terms = [
        [zero_row, swirl_z, -swirl_y],
        [-swirl_z, zero_row, swirl_x],
        [swirl_y, -swirl_x, zero_row],
    ]
    out_rows = [
        biot_scale * kernel_sums[0],
        biot_scale * kernel_sums[1],
        biot_scale * kernel_sums[2],
    ]
    for comp_m in range(3):
        for comp_n in range(3):
            out_rows.append(
                biot_scale
                * (levi_terms[comp_m][comp_n] - 3.0 * kernel_sums[6 + comp_n * 3 + comp_m])
            )
    return jnp.stack(out_rows)


def apply_mask(finished_rows, slot_counts, slot_cap):
    slot_ids = jnp.arange(slot_cap).astype(slot_counts.dtype)
    alive_mask = (slot_ids[None, :] < slot_counts[:, None]).astype(jnp.float32).reshape(-1)
    masked = finished_rows * alive_mask[None, :]
    cell_total = slot_counts.shape[0]
    return (
        masked[0:3].reshape(3, cell_total, slot_cap),
        masked[3:12].reshape(9, cell_total, slot_cap),
    )


def per_device(band_cells, cell_counts, cell_assign, wake_pos, wake_strength, wake_core):
    axes = ("row", "col")
    col_devs = lax.axis_size("col")
    cell_total = band_cells.shape[1]
    slot_cap = band_cells.shape[2]
    group_cells = cell_total * col_devs
    packed = jnp.concatenate(
        [
            band_cells.transpose(1, 0, 2).reshape(cell_total, 3 * slot_cap),
            cell_counts.astype(jnp.float32)[:, None],
            cell_assign.astype(jnp.float32)[:, None],
        ],
        axis=1,
    )
    devices = lax.axis_size("row") * col_devs
    flat = packed.reshape(1, 1, packed.size)
    copies = jnp.broadcast_to(flat, (devices, 1, packed.size))
    sources = spread_sources(wake_pos, wake_strength, wake_core)
    every_cell = lax.all_to_all(copies, axes, 0, 0, tiled=True)
    every_cell, sources = lax.optimization_barrier((every_cell, sources))
    all_cells = devices * cell_total
    every_cell = every_cell.reshape(all_cells, packed.shape[1])
    groups = all_cells // group_cells
    grouped = every_cell.reshape(groups, group_cells, 3 * slot_cap + 2)
    within = grouped[:, :, -1].astype(jnp.int32) % group_cells
    lane = jnp.arange(group_cells * slot_cap, dtype=jnp.int32)
    chosen = within[:, None, :] == (lane // slot_cap)[None, :, None]
    coords = grouped[:, :, : 3 * slot_cap].reshape(groups, group_cells, 3, slot_cap)
    picked = coords[..., 0][..., None]
    for slot in range(1, slot_cap):
        picked = jnp.where((lane % slot_cap) == slot, coords[..., slot][..., None], picked)
    picked = picked.transpose(2, 0, 3, 1)
    target_pos = jnp.sum(jnp.where(chosen[None], picked, 0.0), axis=-1)
    target_pos = target_pos.reshape(3, all_cells * slot_cap)
    device = lax.axis_index("row") * col_devs + lax.axis_index("col")
    own_group = lax.dynamic_index_in_dim(grouped, device // col_devs, 0, keepdims=False)
    own_within = lax.dynamic_index_in_dim(within, device // col_devs, 0, keepdims=False)
    own_slots = (device % col_devs) * cell_total + jnp.arange(cell_total, dtype=jnp.int32)
    own_counts = jnp.sum(
        jnp.where(own_within[None, :] == own_slots[:, None], own_group[None, :, 3 * slot_cap], 0.0),
        axis=1,
    )
    local_sums = pair_sums(target_pos, sources)
    rows = local_sums.shape[0]
    by_device = local_sums.reshape(rows, devices, cell_total * slot_cap).transpose(1, 0, 2)
    own_rows = jnp.sum(lax.all_to_all(by_device, axes, 0, 0, tiled=True), axis=0)
    own_rows = jnp.concatenate([own_rows, -(own_rows[6:7] + own_rows[10:11])], axis=0)
    finished_rows = combine_rows(own_rows)
    return apply_mask(finished_rows, own_counts, slot_cap)


def solution(mesh):
    placed = (
        P(None, ("row", "col"), None),
        P(("row", "col")),
        P(("row", "col")),
        P(None, ("row", "col")),
        P(None, ("row", "col")),
        P(None, ("row", "col")),
    )
    return jax.shard_map(
        per_device,
        mesh=mesh,
        in_specs=placed,
        out_specs=(P(None, ("row", "col"), None), P(None, ("row", "col"), None)),
        check_vma=False,
    )
```

```python
import math

import jax
import jax.numpy as jnp
from jax import lax
from jax.experimental import pallas as pl
from jax.experimental.pallas import tpu as pltpu
from jax.sharding import PartitionSpec as P

HIGHEST = lax.Precision.HIGHEST
ROWS = 14


def block_sums(target_pos, source_pos, source_str, source_core):
    delta_x = target_pos[0][:, None] - source_pos[0][None, :]
    delta_y = target_pos[1][:, None] - source_pos[1][None, :]
    delta_z = target_pos[2][:, None] - source_pos[2][None, :]
    radius_sq = (
        delta_x * delta_x
        + delta_y * delta_y
        + delta_z * delta_z
        + source_core[0][None, :] * source_core[0][None, :]
    )
    inverse = lax.rsqrt(radius_sq)
    kernel_three = inverse * inverse * inverse
    kernel_five = kernel_three * inverse * inverse
    alpha_x = source_str[0][None, :]
    alpha_y = source_str[1][None, :]
    alpha_z = source_str[2][None, :]
    cross_x = delta_y * alpha_z - delta_z * alpha_y
    cross_y = delta_z * alpha_x - delta_x * alpha_z
    cross_z = delta_x * alpha_y - delta_y * alpha_x
    terms_list = [
        kernel_three * cross_x,
        kernel_three * cross_y,
        kernel_three * cross_z,
        kernel_three * alpha_x,
        kernel_three * alpha_y,
        kernel_three * alpha_z,
    ]
    for along in (delta_x, delta_y, delta_z):
        for cross in (cross_x, cross_y, cross_z):
            terms_list.append(kernel_five * along * cross)
    return jnp.stack([jnp.sum(term, axis=1) for term in terms_list])


def pair_kernel(source_ref, target_ref, out_ref, total_ref):
    chunk = source_ref.shape[1]
    shape = target_ref.shape[1:]
    target_x = target_ref[0]
    target_y = target_ref[1]
    target_z = target_ref[2]

    @pl.when(pl.program_id(0) == 0)
    def _():
        total_ref[...] = jnp.zeros_like(total_ref)

    def one_source(index, running):
        def spread(row):
            return jnp.broadcast_to(source_ref[row, pl.ds(index, 1), :], shape)

        delta_x = target_x - spread(0)
        delta_y = target_y - spread(1)
        delta_z = target_z - spread(2)
        alpha_x = spread(3)
        alpha_y = spread(4)
        alpha_z = spread(5)
        radius_sq = delta_x * delta_x + delta_y * delta_y + delta_z * delta_z + spread(6)
        inverse = lax.rsqrt(radius_sq)
        inverse_sq = inverse * inverse
        kernel_three = inverse_sq * inverse
        swirl_x = kernel_three * alpha_x
        swirl_y = kernel_three * alpha_y
        swirl_z = kernel_three * alpha_z
        three_x = delta_y * swirl_z - delta_z * swirl_y
        three_y = delta_z * swirl_x - delta_x * swirl_z
        three_z = delta_x * swirl_y - delta_y * swirl_x
        terms = [three_x, three_y, three_z, swirl_x, swirl_y, swirl_z]
        for along in (delta_x, delta_y, delta_z):
            scaled = inverse_sq * along
            terms.extend([scaled * three_x, scaled * three_y, scaled * three_z])
        return tuple(total + term for total, term in zip(running, terms[:ROWS]))

    start = tuple(total_ref[row] for row in range(ROWS))
    running = lax.fori_loop(0, chunk, one_source, start, unroll=32)
    for row in range(ROWS):
        total_ref[row] = running[row]

    @pl.when(pl.program_id(0) == pl.num_programs(0) - 1)
    def _():
        width = shape[0]
        for row in range(ROWS):
            out_ref[:, 0, row * width : (row + 1) * width] = running[row].T


def spread_sources(source_pos, source_str, source_core):
    sources = jnp.concatenate([source_pos, source_str, source_core * source_core], axis=0)
    return jnp.broadcast_to(sources[:, :, None], sources.shape + (128,))


def pair_sums(targets, sources):
    per_device, devices = targets.shape[1:]
    source_total = sources.shape[1]
    chunk = math.gcd(source_total, 1024)
    return pl.pallas_call(
        pair_kernel,
        grid=(source_total // chunk,),
        in_specs=[
            pl.BlockSpec((7, chunk, 128), lambda step: (0, step, 0)),
            pl.BlockSpec((3, per_device, devices), lambda step: (0, 0, 0)),
        ],
        out_specs=pl.BlockSpec((devices, 1, ROWS * per_device), lambda step: (0, 0, 0)),
        out_shape=jax.ShapeDtypeStruct((devices, 1, ROWS * per_device), jnp.float32),
        scratch_shapes=[pltpu.VMEM((ROWS, per_device, devices), jnp.float32)],
    )(sources, targets)


def combine_rows(kernel_sums):
    biot_scale = -1.0 / (4.0 * math.pi)
    swirl_x, swirl_y, swirl_z = (kernel_sums[3], kernel_sums[4], kernel_sums[5])
    zero_row = jnp.zeros_like(swirl_x)
    levi_terms = [
        [zero_row, swirl_z, -swirl_y],
        [-swirl_z, zero_row, swirl_x],
        [swirl_y, -swirl_x, zero_row],
    ]
    out_rows = [
        biot_scale * kernel_sums[0],
        biot_scale * kernel_sums[1],
        biot_scale * kernel_sums[2],
    ]
    for comp_m in range(3):
        for comp_n in range(3):
            out_rows.append(
                biot_scale
                * (levi_terms[comp_m][comp_n] - 3.0 * kernel_sums[6 + comp_n * 3 + comp_m])
            )
    return jnp.stack(out_rows)


def apply_mask(finished_rows, slot_counts, slot_cap):
    slot_ids = jnp.arange(slot_cap).astype(slot_counts.dtype)
    alive_mask = (slot_ids[None, :] < slot_counts[:, None]).astype(jnp.float32).reshape(-1)
    masked = finished_rows * alive_mask[None, :]
    cell_total = slot_counts.shape[0]
    return (
        masked[0:3].reshape(3, cell_total, slot_cap),
        masked[3:12].reshape(9, cell_total, slot_cap),
    )


def per_device(band_cells, cell_counts, cell_assign, wake_pos, wake_strength, wake_core):
    axes = ("row", "col")
    col_devs = lax.axis_size("col")
    cell_total = band_cells.shape[1]
    slot_cap = band_cells.shape[2]
    group_cells = cell_total * col_devs
    packed = jnp.concatenate(
        [
            band_cells.transpose(1, 0, 2).reshape(cell_total, 3 * slot_cap),
            cell_counts.astype(jnp.float32)[:, None],
            cell_assign.astype(jnp.float32)[:, None],
        ],
        axis=1,
    )
    devices = lax.axis_size("row") * col_devs
    flat = packed.reshape(1, 1, packed.size)
    copies = jnp.broadcast_to(flat, (devices, 1, packed.size))
    sources = spread_sources(wake_pos, wake_strength, wake_core)
    every_cell = lax.all_to_all(copies, axes, 0, 0, tiled=True)
    every_cell, sources = lax.optimization_barrier((every_cell, sources))
    all_cells = devices * cell_total
    every_cell = every_cell.reshape(all_cells, packed.shape[1])
    groups = all_cells // group_cells
    grouped = every_cell.reshape(groups, group_cells, 3 * slot_cap + 2)
    within = grouped[:, :, -1].astype(jnp.int32) % group_cells
    coords = grouped[:, :, : 3 * slot_cap].reshape(groups, group_cells, 3, slot_cap)
    per_device = cell_total * slot_cap
    index = jnp.arange(per_device, dtype=jnp.int32)[:, None]
    peer = jnp.arange(devices, dtype=jnp.int32)[None, :]
    wanted = (peer % col_devs) * cell_total + index // slot_cap
    within_peer = jnp.repeat(within, col_devs, axis=0)
    chosen = within_peer[None, :, :] == wanted[:, :, None]
    coords_peer = jnp.repeat(coords, col_devs, axis=0).transpose(2, 3, 0, 1)
    picked = coords_peer[:, 0][:, None]
    for slot in range(1, slot_cap):
        picked = jnp.where((index % slot_cap == slot)[None, :, :, None], coords_peer[:, slot][:, None], picked)
    target_pos = jnp.sum(jnp.where(chosen[None], picked, 0.0), axis=-1)
    device = lax.axis_index("row") * col_devs + lax.axis_index("col")
    own_group = lax.dynamic_index_in_dim(grouped, device // col_devs, 0, keepdims=False)
    own_within = lax.dynamic_index_in_dim(within, device // col_devs, 0, keepdims=False)
    own_slots = (device % col_devs) * cell_total + jnp.arange(cell_total, dtype=jnp.int32)
    own_counts = jnp.sum(
        jnp.where(own_within[None, :] == own_slots[:, None], own_group[None, :, 3 * slot_cap], 0.0),
        axis=1,
    )
    by_device = pair_sums(target_pos, sources)
    own_rows = jnp.sum(lax.all_to_all(by_device, axes, 0, 0, tiled=True), axis=0)
    own_rows = own_rows.reshape(ROWS, per_device)
    own_rows = jnp.concatenate([own_rows, -(own_rows[6:7] + own_rows[10:11])], axis=0)
    finished_rows = combine_rows(own_rows)
    return apply_mask(finished_rows, own_counts, slot_cap)


def solution(mesh):
    placed = (
        P(None, ("row", "col"), None),
        P(("row", "col")),
        P(("row", "col")),
        P(None, ("row", "col")),
        P(None, ("row", "col")),
        P(None, ("row", "col")),
    )
    return jax.shard_map(
        per_device,
        mesh=mesh,
        in_specs=placed,
        out_specs=(P(None, ("row", "col"), None), P(None, ("row", "col"), None)),
        check_vma=False,
    )
```

```python
import math

import jax
import jax.numpy as jnp
from jax import lax
from jax.experimental import pallas as pl
from jax.experimental.pallas import tpu as pltpu
from jax.sharding import PartitionSpec as P

HIGHEST = lax.Precision.HIGHEST
ROWS = 14


def block_sums(target_pos, source_pos, source_str, source_core):
    delta_x = target_pos[0][:, None] - source_pos[0][None, :]
    delta_y = target_pos[1][:, None] - source_pos[1][None, :]
    delta_z = target_pos[2][:, None] - source_pos[2][None, :]
    radius_sq = (
        delta_x * delta_x
        + delta_y * delta_y
        + delta_z * delta_z
        + source_core[0][None, :] * source_core[0][None, :]
    )
    inverse = lax.rsqrt(radius_sq)
    kernel_three = inverse * inverse * inverse
    kernel_five = kernel_three * inverse * inverse
    alpha_x = source_str[0][None, :]
    alpha_y = source_str[1][None, :]
    alpha_z = source_str[2][None, :]
    cross_x = delta_y * alpha_z - delta_z * alpha_y
    cross_y = delta_z * alpha_x - delta_x * alpha_z
    cross_z = delta_x * alpha_y - delta_y * alpha_x
    terms_list = [
        kernel_three * cross_x,
        kernel_three * cross_y,
        kernel_three * cross_z,
        kernel_three * alpha_x,
        kernel_three * alpha_y,
        kernel_three * alpha_z,
    ]
    for along in (delta_x, delta_y, delta_z):
        for cross in (cross_x, cross_y, cross_z):
            terms_list.append(kernel_five * along * cross)
    return jnp.stack([jnp.sum(term, axis=1) for term in terms_list])


def pair_kernel(source_ref, target_ref, out_ref, total_ref):
    chunk = source_ref.shape[1]
    shape = target_ref.shape[1:]
    target_x = target_ref[0]
    target_y = target_ref[1]
    target_z = target_ref[2]

    @pl.when(pl.program_id(0) == 0)
    def _():
        total_ref[...] = jnp.zeros_like(total_ref)

    def one_source(index, running):
        def spread(row):
            return jnp.broadcast_to(source_ref[row, pl.ds(index, 1), :], shape)

        delta_x = target_x - spread(0)
        delta_y = target_y - spread(1)
        delta_z = target_z - spread(2)
        alpha_x = spread(3)
        alpha_y = spread(4)
        alpha_z = spread(5)
        radius_sq = delta_x * delta_x + delta_y * delta_y + delta_z * delta_z + spread(6)
        inverse = lax.rsqrt(radius_sq)
        inverse_sq = inverse * inverse
        kernel_three = inverse_sq * inverse
        swirl_x = kernel_three * alpha_x
        swirl_y = kernel_three * alpha_y
        swirl_z = kernel_three * alpha_z
        three_x = delta_y * swirl_z - delta_z * swirl_y
        three_y = delta_z * swirl_x - delta_x * swirl_z
        three_z = delta_x * swirl_y - delta_y * swirl_x
        terms = [three_x, three_y, three_z, swirl_x, swirl_y, swirl_z]
        for along in (delta_x, delta_y, delta_z):
            scaled = inverse_sq * along
            terms.extend([scaled * three_x, scaled * three_y, scaled * three_z])
        return tuple(total + term for total, term in zip(running, terms[:ROWS]))

    start = tuple(total_ref[row] for row in range(ROWS))
    running = lax.fori_loop(0, chunk, one_source, start, unroll=32)
    for row in range(ROWS):
        total_ref[row] = running[row]

    @pl.when(pl.program_id(0) == pl.num_programs(0) - 1)
    def _():
        width = shape[0]
        for row in range(ROWS):
            out_ref[:, 0, row * width : (row + 1) * width] = running[row].T


def spread_sources(source_pos, source_str, source_core):
    sources = jnp.concatenate([source_pos, source_str, source_core * source_core], axis=0)
    return jnp.broadcast_to(sources[:, :, None], sources.shape + (128,))


def pair_sums(targets, sources):
    per_device, devices = targets.shape[1:]
    source_total = sources.shape[1]
    chunk = math.gcd(source_total, 1024)
    return pl.pallas_call(
        pair_kernel,
        grid=(source_total // chunk,),
        in_specs=[
            pl.BlockSpec((7, chunk, 128), lambda step: (0, step, 0)),
            pl.BlockSpec((3, per_device, devices), lambda step: (0, 0, 0)),
        ],
        out_specs=pl.BlockSpec((devices, 1, ROWS * per_device), lambda step: (0, 0, 0)),
        out_shape=jax.ShapeDtypeStruct((devices, 1, ROWS * per_device), jnp.float32),
        scratch_shapes=[pltpu.VMEM((ROWS, per_device, devices), jnp.float32)],
    )(sources, targets)


def combine_rows(kernel_sums):
    biot_scale = -1.0 / (4.0 * math.pi)
    swirl_x, swirl_y, swirl_z = (kernel_sums[3], kernel_sums[4], kernel_sums[5])
    zero_row = jnp.zeros_like(swirl_x)
    levi_terms = [
        [zero_row, swirl_z, -swirl_y],
        [-swirl_z, zero_row, swirl_x],
        [swirl_y, -swirl_x, zero_row],
    ]
    out_rows = [
        biot_scale * kernel_sums[0],
        biot_scale * kernel_sums[1],
        biot_scale * kernel_sums[2],
    ]
    for comp_m in range(3):
        for comp_n in range(3):
            out_rows.append(
                biot_scale
                * (levi_terms[comp_m][comp_n] - 3.0 * kernel_sums[6 + comp_n * 3 + comp_m])
            )
    return jnp.stack(out_rows)


def apply_mask(finished_rows, slot_counts, slot_cap):
    slot_ids = jnp.arange(slot_cap).astype(slot_counts.dtype)
    alive_mask = (slot_ids[None, :] < slot_counts[:, None]).astype(jnp.float32).reshape(-1)
    masked = finished_rows * alive_mask[None, :]
    cell_total = slot_counts.shape[0]
    return (
        masked[0:3].reshape(3, cell_total, slot_cap),
        masked[3:12].reshape(9, cell_total, slot_cap),
    )


def per_device(band_cells, cell_counts, cell_assign, wake_pos, wake_strength, wake_core):
    axes = ("row", "col")
    col_devs = lax.axis_size("col")
    cell_total = band_cells.shape[1]
    slot_cap = band_cells.shape[2]
    group_cells = cell_total * col_devs
    packed = jnp.concatenate(
        [
            band_cells.transpose(1, 0, 2).reshape(cell_total, 3 * slot_cap),
            cell_counts.astype(jnp.float32)[:, None],
            cell_assign.astype(jnp.float32)[:, None],
        ],
        axis=1,
    )
    devices = lax.axis_size("row") * col_devs
    flat = packed.reshape(1, 1, packed.size)
    copies = jnp.broadcast_to(flat, (devices, 1, packed.size))
    sources = spread_sources(wake_pos, wake_strength, wake_core)
    every_cell = lax.all_to_all(copies, axes, 0, 0, tiled=True)
    every_cell, sources = lax.optimization_barrier((every_cell, sources))
    all_cells = devices * cell_total
    every_cell = every_cell.reshape(all_cells, packed.shape[1])
    groups = all_cells // group_cells
    grouped = every_cell.reshape(groups, group_cells, 3 * slot_cap + 2)
    within = grouped[:, :, -1].astype(jnp.int32) % group_cells
    coords = grouped[:, :, : 3 * slot_cap].reshape(groups, group_cells, 3, slot_cap)
    per_device = cell_total * slot_cap
    index = jnp.arange(per_device, dtype=jnp.int32)[:, None]
    peer = jnp.arange(devices, dtype=jnp.int32)[None, :]
    wanted = (peer % col_devs) * cell_total + index % cell_total
    within_peer = jnp.repeat(within, col_devs, axis=0)
    chosen = within_peer[None, :, :] == wanted[:, :, None]
    coords_peer = jnp.repeat(coords, col_devs, axis=0).transpose(2, 3, 0, 1)
    picked = coords_peer[:, 0][:, None]
    for slot in range(1, slot_cap):
        picked = jnp.where((index // cell_total == slot)[None, :, :, None], coords_peer[:, slot][:, None], picked)
    target_pos = jnp.sum(jnp.where(chosen[None], picked, 0.0), axis=-1)
    device = lax.axis_index("row") * col_devs + lax.axis_index("col")
    own_group = lax.dynamic_index_in_dim(grouped, device // col_devs, 0, keepdims=False)
    own_within = lax.dynamic_index_in_dim(within, device // col_devs, 0, keepdims=False)
    own_slots = (device % col_devs) * cell_total + jnp.arange(cell_total, dtype=jnp.int32)
    own_counts = jnp.sum(
        jnp.where(own_within[None, :] == own_slots[:, None], own_group[None, :, 3 * slot_cap], 0.0),
        axis=1,
    )
    by_device = pair_sums(target_pos, sources)
    own_rows = jnp.sum(lax.all_to_all(by_device, axes, 0, 0, tiled=True), axis=0)
    own_rows = own_rows.reshape(ROWS, per_device)
    own_rows = jnp.concatenate([own_rows, -(own_rows[6:7] + own_rows[10:11])], axis=0)
    finished_rows = combine_rows(own_rows)
    slot_ids = jnp.arange(slot_cap).astype(own_counts.dtype)
    alive = (slot_ids[:, None] < own_counts[None, :]).astype(jnp.float32)
    velocity = (finished_rows[0:3].reshape(3, slot_cap, cell_total) * alive[None]).transpose(0, 2, 1)
    gradient = (finished_rows[3:12].reshape(9, slot_cap, cell_total) * alive[None]).transpose(0, 2, 1)
    return velocity, gradient


def solution(mesh):
    placed = (
        P(None, ("row", "col"), None),
        P(("row", "col")),
        P(("row", "col")),
        P(None, ("row", "col")),
        P(None, ("row", "col")),
        P(None, ("row", "col")),
    )
    return jax.shard_map(
        per_device,
        mesh=mesh,
        in_specs=placed,
        out_specs=(P(None, ("row", "col"), None), P(None, ("row", "col"), None)),
        check_vma=False,
    )
```

```python
import math

import jax
import jax.numpy as jnp
from jax import lax
from jax.experimental import pallas as pl
from jax.experimental.pallas import tpu as pltpu
from jax.sharding import PartitionSpec as P

HIGHEST = lax.Precision.HIGHEST
ROWS = 14


def block_sums(target_pos, source_pos, source_str, source_core):
    delta_x = target_pos[0][:, None] - source_pos[0][None, :]
    delta_y = target_pos[1][:, None] - source_pos[1][None, :]
    delta_z = target_pos[2][:, None] - source_pos[2][None, :]
    radius_sq = (
        delta_x * delta_x
        + delta_y * delta_y
        + delta_z * delta_z
        + source_core[0][None, :] * source_core[0][None, :]
    )
    inverse = lax.rsqrt(radius_sq)
    kernel_three = inverse * inverse * inverse
    kernel_five = kernel_three * inverse * inverse
    alpha_x = source_str[0][None, :]
    alpha_y = source_str[1][None, :]
    alpha_z = source_str[2][None, :]
    cross_x = delta_y * alpha_z - delta_z * alpha_y
    cross_y = delta_z * alpha_x - delta_x * alpha_z
    cross_z = delta_x * alpha_y - delta_y * alpha_x
    terms_list = [
        kernel_three * cross_x,
        kernel_three * cross_y,
        kernel_three * cross_z,
        kernel_three * alpha_x,
        kernel_three * alpha_y,
        kernel_three * alpha_z,
    ]
    for along in (delta_x, delta_y, delta_z):
        for cross in (cross_x, cross_y, cross_z):
            terms_list.append(kernel_five * along * cross)
    return jnp.stack([jnp.sum(term, axis=1) for term in terms_list])


def pair_kernel(source_ref, target_ref, out_ref, total_ref):
    chunk = source_ref.shape[1]
    shape = target_ref.shape[1:]
    target_x = target_ref[0]
    target_y = target_ref[1]
    target_z = target_ref[2]

    @pl.when(pl.program_id(0) == 0)
    def _():
        total_ref[...] = jnp.zeros_like(total_ref)

    def one_source(index, running):
        def spread(row):
            return jnp.broadcast_to(source_ref[row, pl.ds(index, 1), :], shape)

        delta_x = target_x - spread(0)
        delta_y = target_y - spread(1)
        delta_z = target_z - spread(2)
        alpha_x = spread(3)
        alpha_y = spread(4)
        alpha_z = spread(5)
        radius_sq = delta_x * delta_x + delta_y * delta_y + delta_z * delta_z + spread(6)
        inverse = lax.rsqrt(radius_sq)
        inverse_sq = inverse * inverse
        kernel_three = inverse_sq * inverse
        swirl_x = kernel_three * alpha_x
        swirl_y = kernel_three * alpha_y
        swirl_z = kernel_three * alpha_z
        three_x = delta_y * swirl_z - delta_z * swirl_y
        three_y = delta_z * swirl_x - delta_x * swirl_z
        three_z = delta_x * swirl_y - delta_y * swirl_x
        terms = [three_x, three_y, three_z, swirl_x, swirl_y, swirl_z]
        for along in (delta_x, delta_y, delta_z):
            scaled = inverse_sq * along
            terms.extend([scaled * three_x, scaled * three_y, scaled * three_z])
        return tuple(total + term for total, term in zip(running, terms[:ROWS]))

    start = tuple(total_ref[row] for row in range(ROWS))
    running = lax.fori_loop(0, chunk, one_source, start, unroll=32)
    for row in range(ROWS):
        total_ref[row] = running[row]

    @pl.when(pl.program_id(0) == pl.num_programs(0) - 1)
    def _():
        width = shape[0]
        for row in range(ROWS):
            out_ref[:, 0, row * width : (row + 1) * width] = running[row].T


def spread_sources(source_pos, source_str, source_core):
    sources = jnp.concatenate([source_pos, source_str, source_core * source_core], axis=0)
    return jnp.broadcast_to(sources[:, :, None], sources.shape + (128,))


def pair_sums(targets, sources):
    per_device, devices = targets.shape[1:]
    source_total = sources.shape[1]
    chunk = math.gcd(source_total, 1024)
    return pl.pallas_call(
        pair_kernel,
        grid=(source_total // chunk,),
        in_specs=[
            pl.BlockSpec((7, chunk, 128), lambda step: (0, step, 0)),
            pl.BlockSpec((3, per_device, devices), lambda step: (0, 0, 0)),
        ],
        out_specs=pl.BlockSpec((devices, 1, ROWS * per_device), lambda step: (0, 0, 0)),
        out_shape=jax.ShapeDtypeStruct((devices, 1, ROWS * per_device), jnp.float32),
        scratch_shapes=[pltpu.VMEM((ROWS, per_device, devices), jnp.float32)],
    )(sources, targets)


def combine_rows(kernel_sums):
    biot_scale = -1.0 / (4.0 * math.pi)
    swirl_x, swirl_y, swirl_z = (kernel_sums[3], kernel_sums[4], kernel_sums[5])
    zero_row = jnp.zeros_like(swirl_x)
    levi_terms = [
        [zero_row, swirl_z, -swirl_y],
        [-swirl_z, zero_row, swirl_x],
        [swirl_y, -swirl_x, zero_row],
    ]
    out_rows = [
        biot_scale * kernel_sums[0],
        biot_scale * kernel_sums[1],
        biot_scale * kernel_sums[2],
    ]
    for comp_m in range(3):
        for comp_n in range(3):
            out_rows.append(
                biot_scale
                * (levi_terms[comp_m][comp_n] - 3.0 * kernel_sums[6 + comp_n * 3 + comp_m])
            )
    return jnp.stack(out_rows)


def apply_mask(finished_rows, slot_counts, slot_cap):
    slot_ids = jnp.arange(slot_cap).astype(slot_counts.dtype)
    alive_mask = (slot_ids[None, :] < slot_counts[:, None]).astype(jnp.float32).reshape(-1)
    masked = finished_rows * alive_mask[None, :]
    cell_total = slot_counts.shape[0]
    return (
        masked[0:3].reshape(3, cell_total, slot_cap),
        masked[3:12].reshape(9, cell_total, slot_cap),
    )


def per_device(band_cells, cell_counts, cell_assign, wake_pos, wake_strength, wake_core):
    axes = ("row", "col")
    col_devs = lax.axis_size("col")
    cell_total = band_cells.shape[1]
    slot_cap = band_cells.shape[2]
    group_cells = cell_total * col_devs
    packed = jnp.concatenate(
        [
            band_cells.transpose(1, 0, 2).reshape(cell_total, 3 * slot_cap),
            cell_counts.astype(jnp.float32)[:, None],
            cell_assign.astype(jnp.float32)[:, None],
        ],
        axis=1,
    )
    devices = lax.axis_size("row") * col_devs
    flat = packed.reshape(1, 1, packed.size)
    copies = jnp.broadcast_to(flat, (devices, 1, packed.size))
    sources = spread_sources(wake_pos, wake_strength, wake_core)
    every_cell = lax.all_to_all(copies, axes, 0, 0, tiled=True)
    every_cell, sources = lax.optimization_barrier((every_cell, sources))
    all_cells = devices * cell_total
    every_cell = every_cell.reshape(all_cells, packed.shape[1])
    groups = all_cells // group_cells
    grouped = every_cell.reshape(groups, group_cells, 3 * slot_cap + 2)
    within = grouped[:, :, -1].astype(jnp.int32) % group_cells
    coords = grouped[:, :, : 3 * slot_cap].reshape(groups, group_cells, 3, slot_cap)
    per_device = cell_total * slot_cap
    index = jnp.arange(per_device, dtype=jnp.int32)[:, None]
    member = jnp.arange(col_devs, dtype=jnp.int32)[None, :]
    wanted = member * cell_total + index % cell_total
    chosen = within[None, :, None, :] == wanted[:, None, :, None]
    coords_slot = coords.transpose(2, 3, 0, 1)
    picked = coords_slot[:, 0][:, None, :, None, :]
    for slot in range(1, slot_cap):
        picked = jnp.where(
            (index // cell_total == slot)[None, :, :, None, None][:, :, :1],
            coords_slot[:, slot][:, None, :, None, :],
            picked,
        )
    target_pos = jnp.sum(jnp.where(chosen[None], picked, 0.0), axis=-1)
    target_pos = target_pos.reshape(3, per_device, devices)
    device = lax.axis_index("row") * col_devs + lax.axis_index("col")
    own_group = lax.dynamic_index_in_dim(grouped, device // col_devs, 0, keepdims=False)
    own_within = lax.dynamic_index_in_dim(within, device // col_devs, 0, keepdims=False)
    own_slots = (device % col_devs) * cell_total + jnp.arange(cell_total, dtype=jnp.int32)
    own_counts = jnp.sum(
        jnp.where(own_within[None, :] == own_slots[:, None], own_group[None, :, 3 * slot_cap], 0.0),
        axis=1,
    )
    by_device = pair_sums(target_pos, sources)
    own_rows = jnp.sum(lax.all_to_all(by_device, axes, 0, 0, tiled=True), axis=0)
    own_rows = own_rows.reshape(ROWS, per_device)
    own_rows = jnp.concatenate([own_rows, -(own_rows[6:7] + own_rows[10:11])], axis=0)
    finished_rows = combine_rows(own_rows)
    slot_ids = jnp.arange(slot_cap).astype(own_counts.dtype)
    alive = (slot_ids[:, None] < own_counts[None, :]).astype(jnp.float32)
    velocity = (finished_rows[0:3].reshape(3, slot_cap, cell_total) * alive[None]).transpose(0, 2, 1)
    gradient = (finished_rows[3:12].reshape(9, slot_cap, cell_total) * alive[None]).transpose(0, 2, 1)
    return velocity, gradient


def solution(mesh):
    placed = (
        P(None, ("row", "col"), None),
        P(("row", "col")),
        P(("row", "col")),
        P(None, ("row", "col")),
        P(None, ("row", "col")),
        P(None, ("row", "col")),
    )
    return jax.shard_map(
        per_device,
        mesh=mesh,
        in_specs=placed,
        out_specs=(P(None, ("row", "col"), None), P(None, ("row", "col"), None)),
        check_vma=False,
    )
```

```python
import math

import jax
import jax.numpy as jnp
from jax import lax
from jax.experimental import pallas as pl
from jax.experimental.pallas import tpu as pltpu
from jax.sharding import PartitionSpec as P

HIGHEST = lax.Precision.HIGHEST
ROWS = 14


def block_sums(target_pos, source_pos, source_str, source_core):
    delta_x = target_pos[0][:, None] - source_pos[0][None, :]
    delta_y = target_pos[1][:, None] - source_pos[1][None, :]
    delta_z = target_pos[2][:, None] - source_pos[2][None, :]
    radius_sq = (
        delta_x * delta_x
        + delta_y * delta_y
        + delta_z * delta_z
        + source_core[0][None, :] * source_core[0][None, :]
    )
    inverse = lax.rsqrt(radius_sq)
    kernel_three = inverse * inverse * inverse
    kernel_five = kernel_three * inverse * inverse
    alpha_x = source_str[0][None, :]
    alpha_y = source_str[1][None, :]
    alpha_z = source_str[2][None, :]
    cross_x = delta_y * alpha_z - delta_z * alpha_y
    cross_y = delta_z * alpha_x - delta_x * alpha_z
    cross_z = delta_x * alpha_y - delta_y * alpha_x
    terms_list = [
        kernel_three * cross_x,
        kernel_three * cross_y,
        kernel_three * cross_z,
        kernel_three * alpha_x,
        kernel_three * alpha_y,
        kernel_three * alpha_z,
    ]
    for along in (delta_x, delta_y, delta_z):
        for cross in (cross_x, cross_y, cross_z):
            terms_list.append(kernel_five * along * cross)
    return jnp.stack([jnp.sum(term, axis=1) for term in terms_list])


def pair_kernel(source_ref, target_ref, out_ref, total_ref):
    chunk = source_ref.shape[1]
    shape = target_ref.shape[1:]
    target_x = target_ref[0]
    target_y = target_ref[1]
    target_z = target_ref[2]

    @pl.when(pl.program_id(0) == 0)
    def _():
        total_ref[...] = jnp.zeros_like(total_ref)

    def one_source(index, running):
        def spread(row):
            return jnp.broadcast_to(source_ref[row, pl.ds(index, 1), :], shape)

        delta_x = target_x - spread(0)
        delta_y = target_y - spread(1)
        delta_z = target_z - spread(2)
        alpha_x = spread(3)
        alpha_y = spread(4)
        alpha_z = spread(5)
        radius_sq = delta_x * delta_x + delta_y * delta_y + delta_z * delta_z + spread(6)
        inverse = lax.rsqrt(radius_sq)
        inverse_sq = inverse * inverse
        kernel_three = inverse_sq * inverse
        swirl_x = kernel_three * alpha_x
        swirl_y = kernel_three * alpha_y
        swirl_z = kernel_three * alpha_z
        three_x = delta_y * swirl_z - delta_z * swirl_y
        three_y = delta_z * swirl_x - delta_x * swirl_z
        three_z = delta_x * swirl_y - delta_y * swirl_x
        terms = [three_x, three_y, three_z, swirl_x, swirl_y, swirl_z]
        for along in (delta_x, delta_y, delta_z):
            scaled = inverse_sq * along
            terms.extend([scaled * three_x, scaled * three_y, scaled * three_z])
        return tuple(total + term for total, term in zip(running, terms[:ROWS]))

    start = tuple(total_ref[row] for row in range(ROWS))
    running = lax.fori_loop(0, chunk, one_source, start, unroll=32)
    for row in range(ROWS):
        total_ref[row] = running[row]

    @pl.when(pl.program_id(0) == pl.num_programs(0) - 1)
    def _():
        width = shape[0]
        for row in range(ROWS):
            out_ref[:, 0, row * width : (row + 1) * width] = running[row].T


def spread_sources(source_pos, source_str, source_core):
    sources = jnp.concatenate([source_pos, source_str, source_core * source_core], axis=0)
    return jnp.broadcast_to(sources[:, :, None], sources.shape + (128,))


def pair_sums(targets, sources):
    per_device, devices = targets.shape[1:]
    source_total = sources.shape[1]
    chunk = math.gcd(source_total, 512)
    return pl.pallas_call(
        pair_kernel,
        grid=(source_total // chunk,),
        in_specs=[
            pl.BlockSpec((7, chunk, 128), lambda step: (0, step, 0)),
            pl.BlockSpec((3, per_device, devices), lambda step: (0, 0, 0)),
        ],
        out_specs=pl.BlockSpec((devices, 1, ROWS * per_device), lambda step: (0, 0, 0)),
        out_shape=jax.ShapeDtypeStruct((devices, 1, ROWS * per_device), jnp.float32),
        scratch_shapes=[pltpu.VMEM((ROWS, per_device, devices), jnp.float32)],
    )(sources, targets)


def combine_rows(kernel_sums):
    biot_scale = -1.0 / (4.0 * math.pi)
    swirl_x, swirl_y, swirl_z = (kernel_sums[3], kernel_sums[4], kernel_sums[5])
    zero_row = jnp.zeros_like(swirl_x)
    levi_terms = [
        [zero_row, swirl_z, -swirl_y],
        [-swirl_z, zero_row, swirl_x],
        [swirl_y, -swirl_x, zero_row],
    ]
    out_rows = [
        biot_scale * kernel_sums[0],
        biot_scale * kernel_sums[1],
        biot_scale * kernel_sums[2],
    ]
    for comp_m in range(3):
        for comp_n in range(3):
            out_rows.append(
                biot_scale
                * (levi_terms[comp_m][comp_n] - 3.0 * kernel_sums[6 + comp_n * 3 + comp_m])
            )
    return jnp.stack(out_rows)


def apply_mask(finished_rows, slot_counts, slot_cap):
    slot_ids = jnp.arange(slot_cap).astype(slot_counts.dtype)
    alive_mask = (slot_ids[None, :] < slot_counts[:, None]).astype(jnp.float32).reshape(-1)
    masked = finished_rows * alive_mask[None, :]
    cell_total = slot_counts.shape[0]
    return (
        masked[0:3].reshape(3, cell_total, slot_cap),
        masked[3:12].reshape(9, cell_total, slot_cap),
    )


def per_device(band_cells, cell_counts, cell_assign, wake_pos, wake_strength, wake_core):
    axes = ("row", "col")
    col_devs = lax.axis_size("col")
    cell_total = band_cells.shape[1]
    slot_cap = band_cells.shape[2]
    group_cells = cell_total * col_devs
    packed = jnp.concatenate(
        [
            band_cells.transpose(1, 0, 2).reshape(cell_total, 3 * slot_cap),
            cell_counts.astype(jnp.float32)[:, None],
            cell_assign.astype(jnp.float32)[:, None],
        ],
        axis=1,
    )
    devices = lax.axis_size("row") * col_devs
    flat = packed.reshape(1, 1, packed.size)
    copies = jnp.broadcast_to(flat, (devices, 1, packed.size))
    sources = spread_sources(wake_pos, wake_strength, wake_core)
    every_cell = lax.all_to_all(copies, axes, 0, 0, tiled=True)
    every_cell, sources = lax.optimization_barrier((every_cell, sources))
    all_cells = devices * cell_total
    every_cell = every_cell.reshape(all_cells, packed.shape[1])
    groups = all_cells // group_cells
    grouped = every_cell.reshape(groups, group_cells, 3 * slot_cap + 2)
    within = grouped[:, :, -1].astype(jnp.int32) % group_cells
    coords = grouped[:, :, : 3 * slot_cap].reshape(groups, group_cells, 3, slot_cap)
    per_device = cell_total * slot_cap
    index = jnp.arange(per_device, dtype=jnp.int32)[:, None]
    peer = jnp.arange(devices, dtype=jnp.int32)[None, :]
    wanted = (peer % col_devs) * cell_total + index % cell_total
    within_peer = jnp.repeat(within, col_devs, axis=0)
    chosen = within_peer[None, :, :] == wanted[:, :, None]
    coords_peer = jnp.repeat(coords, col_devs, axis=0).transpose(2, 3, 0, 1)
    picked = coords_peer[:, 0][:, None]
    for slot in range(1, slot_cap):
        picked = jnp.where((index // cell_total == slot)[None, :, :, None], coords_peer[:, slot][:, None], picked)
    target_pos = jnp.sum(jnp.where(chosen[None], picked, 0.0), axis=-1)
    device = lax.axis_index("row") * col_devs + lax.axis_index("col")
    own_group = lax.dynamic_index_in_dim(grouped, device // col_devs, 0, keepdims=False)
    own_within = lax.dynamic_index_in_dim(within, device // col_devs, 0, keepdims=False)
    own_slots = (device % col_devs) * cell_total + jnp.arange(cell_total, dtype=jnp.int32)
    own_counts = jnp.sum(
        jnp.where(own_within[None, :] == own_slots[:, None], own_group[None, :, 3 * slot_cap], 0.0),
        axis=1,
    )
    by_device = pair_sums(target_pos, sources)
    own_rows = jnp.sum(lax.all_to_all(by_device, axes, 0, 0, tiled=True), axis=0)
    own_rows = own_rows.reshape(ROWS, per_device)
    own_rows = jnp.concatenate([own_rows, -(own_rows[6:7] + own_rows[10:11])], axis=0)
    finished_rows = combine_rows(own_rows)
    slot_ids = jnp.arange(slot_cap).astype(own_counts.dtype)
    alive = (slot_ids[:, None] < own_counts[None, :]).astype(jnp.float32)
    velocity = (finished_rows[0:3].reshape(3, slot_cap, cell_total) * alive[None]).transpose(0, 2, 1)
    gradient = (finished_rows[3:12].reshape(9, slot_cap, cell_total) * alive[None]).transpose(0, 2, 1)
    return velocity, gradient


def solution(mesh):
    placed = (
        P(None, ("row", "col"), None),
        P(("row", "col")),
        P(("row", "col")),
        P(None, ("row", "col")),
        P(None, ("row", "col")),
        P(None, ("row", "col")),
    )
    return jax.shard_map(
        per_device,
        mesh=mesh,
        in_specs=placed,
        out_specs=(P(None, ("row", "col"), None), P(None, ("row", "col"), None)),
        check_vma=False,
    )
```
